256 devices in a mesh: row: 32 (over x, y, core), col: 8 (over z).
Axes of the slice: x: 4, y: 4, z: 8, core: 2. Of those that a mesh axis runs over, the one named last changes fastest.
Arguments:
- features: bfloat16 [8192, 1024], P('row', 'col'), may hold values from -6 to 6
- grad_out: bfloat16 [8192, 1024], P('row', 'col'), may hold values from -6 to 6
- weight: bfloat16 [1024, 1024], replicated, may hold values from -0.1875 to 0.1875
- root_weight: bfloat16 [1024, 1024], replicated, may hold values from -0.1875 to 0.1875
- values: bfloat16 [32, 8, 8, 128, 128], P('row', 'col'), may hold values from -0.125 to 0.125
- positions: int32 [32, 8, 8], P('row', 'col'), may hold values from 0 to 15, as said below
- counts: int32 [32, 8], P('row', 'col'), may hold values from 1 to 8, as said below
Outputs:
- activations: bfloat16 [8192, 1024], P('row', 'col')
- feature_grad: float32 [8192, 1024], P('row', 'col')
- weight_grad: float32 [1024, 1024], P('col')
- root_grad: float32 [1024, 1024], P('col')
The draws below stay inside these ranges and needn't reach their ends.
Inputs may be any that keep to these rules, and one draw needn't show every extreme that they name: Within the first counts slots of a tile the positions are distinct; position p is block row p // 8 and block column p % 8 of the tile. `counts`: some tile uses all 8 slots in every draw; about a quarter of the block rows have much fuller tiles (4 or 8 used slots) than the rest (1 or 2).
All inputs are finite; a program needn't handle non-finite values.
Results may differ from the reference program's by a relative error of at most 0.012.
Values may be sent and summed in bfloat16 or wider, within the bound.
No kernel may reach another device: no remote copies, remote signals or barrier semaphores. Data moves between devices by JAX's collectives and lax.ppermute only.
A program may use at most 64 MiB of HBM per device.

```python
import math
import jax
import jax.numpy as jnp
from jax import lax

FEAT = 1024
BLK = 128
ROWS_DEV = 256
NODES = 8192
RBLK = 2
CBLK = 8
SLOTS = 8
N_ROW = 32
N_COL = 8


def draw_positions(key, part):
    tile_rows = NODES // ROWS_DEV
    tile_cols = NODES // (CBLK * BLK)
    tile_keys = jax.random.split(key, tile_rows * tile_cols)

    def shuffle_one(one_key):
        return jax.random.permutation(one_key, RBLK * CBLK)[:SLOTS]
    shuffled = jax.vmap(shuffle_one)(tile_keys)
    return shuffled.reshape(tile_rows, tile_cols, SLOTS).astype(jnp.int32)


def draw_counts(key, part):
    tile_rows = NODES // ROWS_DEV
    tile_cols = NODES // (CBLK * BLK)
    lower = max(1, SLOTS // 8)
    upper = max(lower + 1, SLOTS // 4 + 1)
    base_count = jax.random.randint(jax.random.fold_in(key, 1), (tile_rows, tile_cols), lower, upper)
    heavy_rows = jax.random.randint(jax.random.fold_in(key, 2), (tile_rows, 1), 0, 4)
    factor = jnp.where(heavy_rows == 0, 4, 1)
    filled = jnp.minimum(base_count * factor, SLOTS)
    chosen_tile = jax.random.randint(jax.random.fold_in(key, 3), (), 0, tile_rows * tile_cols)
    filled = filled.reshape(-1).at[chosen_tile].set(SLOTS).reshape(tile_rows, tile_cols)
    return filled.astype(jnp.int32)


def steps_of(own_key, shape, pieces, low, high):
    def one(axis_at, blocks):
        heights = jax.random.uniform(jax.random.fold_in(jax.random.fold_in(own_key, 6), axis_at), (blocks,), jnp.float32, low / len(pieces), high / len(pieces))
        return jnp.repeat(jnp.exp(heights), shape[axis_at] // blocks).reshape((-1,) + (1,) * (len(shape) - axis_at - 1))

    gain = one(*pieces[0])
    for cut in pieces[1:]:
        gain = gain * one(*cut)
    return gain


def scatter_about(own_key, extent, deviation, reach, pieces=(), held_as=jnp.bfloat16):
    values = jax.random.normal(own_key, extent, jnp.float32) * deviation
    if len(pieces) > 0:
        values = steps_of(own_key, extent, pieces, -0.22, 0.18) * values
    return jnp.clip(values, min=-reach, max=reach).astype(held_as)


def setup_inputs(seed: int = 0) -> dict:
    keys = jax.random.split(jax.random.key(seed), 8)
    return {
        "features": scatter_about(keys[0], (NODES, FEAT), 1.0, 6.0, ((0, 32), (1, 8))),
        "grad_out": scatter_about(keys[1], (NODES, FEAT), 1.0, 6.0, ((0, 32), (1, 8))),
        "weight": scatter_about(keys[2], (FEAT, FEAT), FEAT ** -0.5, 0.1875),
        "root_weight": scatter_about(keys[3], (FEAT, FEAT), FEAT ** -0.5, 0.1875),
        "values": scatter_about(keys[4], (N_ROW, N_COL, SLOTS, BLK, BLK), (2.0 / (NODES // CBLK * SLOTS) ** 0.5), 0.125, ((0, 32), (1, 8))),
        "positions": draw_positions(jax.random.fold_in(keys[7], 71), 0),
        "counts": draw_counts(jax.random.fold_in(keys[7], 71), 0),
    }


def silu_grad(preact):
    sig = jax.nn.sigmoid(preact)
    return sig * (1.0 + preact * (1.0 - sig))

def reference(features, grad_out, weight, root_weight, values, positions, counts):
    slot_index = jnp.arange(SLOTS, dtype=jnp.int32)
    live_mask = (slot_index[None, None, :] < counts[:, :, None]).astype(jnp.float32)
    tile_col = jnp.arange(N_COL, dtype=jnp.int32)[None, :, None] * CBLK
    col_block = (tile_col + positions % CBLK).astype(jnp.int32)
    row_block = (positions // CBLK).astype(jnp.int32)
    feat_blocks = features.reshape(NODES // BLK, BLK, FEAT)

    def forward_row(inputs):
        slot_vals, cols_here, rows_here, live_here = inputs
        slot_vals = slot_vals.reshape(-1, BLK, BLK).astype(jnp.float32)
        picked = feat_blocks[cols_here.reshape(-1)].astype(jnp.float32)
        products = jnp.einsum('sij,sjf->sif', slot_vals, picked) * live_here.reshape(-1)[:, None, None]
        return jax.ops.segment_sum(products, rows_here.reshape(-1), num_segments=RBLK)
    gathered = lax.map(forward_row, (values, col_block, row_block, live_mask))
    aggregated = gathered.reshape(NODES, FEAT).astype(jnp.bfloat16)
    preact = jnp.dot(aggregated, weight, preferred_element_type=jnp.float32) + jnp.dot(features, root_weight, preferred_element_type=jnp.float32)
    activations = jax.nn.silu(preact).astype(jnp.bfloat16)
    preact_grad = (grad_out.astype(jnp.float32) * silu_grad(preact)).astype(jnp.bfloat16)
    grad_scale = 1.0 / math.sqrt(NODES)
    weight_grad = jnp.dot(aggregated.T, preact_grad, preferred_element_type=jnp.float32) * grad_scale
    root_grad = jnp.dot(features.T, preact_grad, preferred_element_type=jnp.float32) * grad_scale
    aggregated_grad = jnp.dot(preact_grad, weight.T, preferred_element_type=jnp.float32).astype(jnp.bfloat16)
    grad_blocks = aggregated_grad.reshape(NODES // BLK, BLK, FEAT)

    def backward_row(running, inputs):
        tile_row, slot_vals, cols_here, rows_here, live_here = inputs
        slot_vals = slot_vals.reshape(-1, BLK, BLK).astype(jnp.float32)
        picked = grad_blocks[(tile_row * RBLK + rows_here.reshape(-1)).astype(jnp.int32)].astype(jnp.float32)
        products = jnp.einsum('sji,sjf->sif', slot_vals, picked) * live_here.reshape(-1)[:, None, None]
        return (running + jax.ops.segment_sum(products, cols_here.reshape(-1), num_segments=NODES // BLK), None)
    running, _ = lax.scan(backward_row, jnp.zeros((NODES // BLK, BLK, FEAT), jnp.float32), (jnp.arange(N_ROW, dtype=jnp.int32), values, col_block, row_block, live_mask))
    feature_grad = running.reshape(NODES, FEAT) + jnp.dot(preact_grad, root_weight.T, preferred_element_type=jnp.float32)
    return (activations, feature_grad, weight_grad, root_grad)
```

```python
import math

import jax
import jax.numpy as jnp
from jax import lax
from jax.sharding import PartitionSpec as P


def silu_grad(preact):
    sig = jax.nn.sigmoid(preact)
    return sig * (1.0 + preact * (1.0 - sig))


def gather_rows(block, axis_name, parts):
    spread = jnp.broadcast_to(block[None], (parts,) + block.shape)
    got = lax.all_to_all(spread, axis_name, 0, 0, tiled=True)
    return got.reshape((parts * block.shape[0],) + block.shape[1:])


def reduce_rows(block, axis_name, parts):
    pieces = block.reshape((parts, block.shape[0] // parts) + block.shape[1:])
    got = lax.all_to_all(pieces, axis_name, 0, 0, tiled=True)
    return got.astype(jnp.float32).sum(0)


def per_device(features, grad_out, weight, root_weight, values, positions, counts):
    node_rows, feat_dev = features.shape
    slots, block_edge = values.shape[2], values.shape[-1]
    row_blocks = node_rows // block_edge
    col_count = lax.axis_size("col")
    row_count = lax.axis_size("row")
    col_index = lax.axis_index("col")

    live = (jnp.arange(slots, dtype=jnp.int32) < counts[0, 0]).astype(values.dtype)
    own_vals = (values[0, 0] * live[:, None, None]).reshape(slots * block_edge, block_edge)
    pos_row = jnp.zeros((16, block_edge), values.dtype)
    pos_row = lax.dynamic_update_slice(
        pos_row, positions[0, 0].astype(values.dtype).reshape(1, slots), (0, 0)
    )
    packed = jnp.concatenate([own_vals, pos_row], axis=0)
    all_packed = lax.all_gather(packed, "col", axis=0, tiled=True).reshape(
        col_count, slots * block_edge + 16, block_edge
    )
    tile_vals = all_packed[:, : slots * block_edge].reshape(
        col_count, slots, block_edge, block_edge
    )
    tile_pos = all_packed[:, slots * block_edge, :slots].astype(jnp.int32)
    cb = row_count * node_rows // col_count // block_edge
    n_pos = row_blocks * cb
    onehot = (tile_pos[:, :, None] == jnp.arange(n_pos, dtype=jnp.int32)[None, None, :]).astype(
        values.dtype
    )
    dense = jnp.einsum(
        "tsp,tsij->tpij", onehot, tile_vals, preferred_element_type=jnp.float32
    ).astype(values.dtype)
    dense = dense.reshape(col_count, row_blocks, cb, block_edge, block_edge)

    x_all = gather_rows(features, "row", row_count)
    x_tiles = x_all.reshape(col_count, cb, block_edge, feat_dev)
    agg_f32 = jnp.einsum("trcij,tcjf->rif", dense, x_tiles, preferred_element_type=jnp.float32)
    aggregated = agg_f32.reshape(node_rows, feat_dev).astype(jnp.bfloat16)

    agg_full = lax.all_gather(aggregated, "col", axis=1, tiled=True)
    feat_full = lax.all_gather(features, "col", axis=1, tiled=True)
    grad_full = lax.all_gather(grad_out, "col", axis=1, tiled=True)
    preact = jnp.dot(agg_full, weight, preferred_element_type=jnp.float32) + jnp.dot(
        feat_full, root_weight, preferred_element_type=jnp.float32
    )
    preact_own = lax.dynamic_slice_in_dim(preact, col_index * feat_dev, feat_dev, 1)
    activations = jax.nn.silu(preact_own).astype(jnp.bfloat16)
    preact_grad = (grad_full.astype(jnp.float32) * silu_grad(preact)).astype(jnp.bfloat16)

    contract_rows = (((0,), (0,)), ((), ()))
    weight_part = lax.dot_general(
        aggregated, preact_grad, contract_rows, preferred_element_type=jnp.float32
    )
    root_part = lax.dot_general(
        features, preact_grad, contract_rows, preferred_element_type=jnp.float32
    )
    both = jnp.concatenate([weight_part, root_part], axis=0)
    both_sum = reduce_rows(both, "row", row_count)
    both_all = gather_rows(both_sum, "row", row_count)
    nodes = row_count * node_rows
    grad_scale = 1.0 / math.sqrt(nodes)
    weight_sum = both_all[:feat_dev]
    root_sum = both_all[feat_dev:]

    w_rows = lax.dynamic_slice_in_dim(weight, col_index * feat_dev, feat_dev, 0)
    r_rows = lax.dynamic_slice_in_dim(root_weight, col_index * feat_dev, feat_dev, 0)
    contract_cols = (((1,), (1,)), ((), ()))
    aggregated_grad = lax.dot_general(
        preact_grad, w_rows, contract_cols, preferred_element_type=jnp.float32
    ).astype(jnp.bfloat16)
    own_grad = lax.dot_general(
        preact_grad, r_rows, contract_cols, preferred_element_type=jnp.float32
    )
    g_rows = aggregated_grad.reshape(row_blocks, block_edge, feat_dev)
    column_terms = jnp.einsum(
        "trcij,rif->tcjf", dense, g_rows, preferred_element_type=jnp.float32
    ).reshape(nodes, feat_dev)
    summed_cols = reduce_rows(column_terms.astype(jnp.bfloat16), "row", row_count)
    feature_grad = summed_cols + own_grad
    return (activations, feature_grad, weight_sum * grad_scale, root_sum * grad_scale)


def solution(mesh):
    in_specs = (
        P("row", "col"),
        P("row", "col"),
        P(),
        P(),
        P("row", "col", None, None, None),
        P("row", "col", None),
        P("row", "col"),
    )
    out_specs = (P("row", "col"), P("row", "col"), P("col", None), P("col", None))
    return jax.shard_map(
        per_device, mesh=mesh, in_specs=in_specs, out_specs=out_specs, check_vma=False
    )
```

```python
import math

import jax
import jax.numpy as jnp
from jax import lax
from jax.sharding import PartitionSpec as P


def silu_grad(preact):
    sig = jax.nn.sigmoid(preact)
    return sig * (1.0 + preact * (1.0 - sig))


def gather_rows(block, axis_name, parts):
    spread = jnp.broadcast_to(block[None], (parts,) + block.shape)
    got = lax.all_to_all(spread, axis_name, 0, 0, tiled=True)
    return got.reshape((parts * block.shape[0],) + block.shape[1:])


def reduce_rows(block, axis_name, parts):
    pieces = block.reshape((parts, block.shape[0] // parts) + block.shape[1:])
    got = lax.all_to_all(pieces, axis_name, 0, 0, tiled=True)
    return got.astype(jnp.float32).sum(0)


def per_device(features, grad_out, weight, root_weight, values, positions, counts):
    node_rows, feat_dev = features.shape
    slots, block_edge = values.shape[2], values.shape[-1]
    row_blocks = node_rows // block_edge
    col_count = lax.axis_size("col")
    row_count = lax.axis_size("row")
    col_index = lax.axis_index("col")

    live = (jnp.arange(slots, dtype=jnp.int32) < counts[0, 0]).astype(values.dtype)
    own_vals = (values[0, 0] * live[:, None, None]).reshape(slots * block_edge, block_edge)
    pos_row = jnp.zeros((16, block_edge), values.dtype)
    pos_row = lax.dynamic_update_slice(
        pos_row, positions[0, 0].astype(values.dtype).reshape(1, slots), (0, 0)
    )
    packed = jnp.concatenate([own_vals, pos_row], axis=0)
    all_packed = lax.all_gather(packed, "col", axis=0, tiled=True).reshape(
        col_count, slots * block_edge + 16, block_edge
    )
    tile_vals = all_packed[:, : slots * block_edge].reshape(
        col_count, slots, block_edge, block_edge
    )
    tile_pos = all_packed[:, slots * block_edge, :slots].astype(jnp.int32)
    cb = row_count * node_rows // col_count // block_edge
    n_pos = row_blocks * cb
    onehot = (tile_pos[:, :, None] == jnp.arange(n_pos, dtype=jnp.int32)[None, None, :]).astype(
        values.dtype
    )
    dense = jnp.einsum(
        "tsp,tsij->tpij", onehot, tile_vals, preferred_element_type=jnp.float32
    ).astype(values.dtype)
    dense = dense.reshape(col_count, row_blocks, cb, block_edge, block_edge)

    x_all = gather_rows(features, "row", row_count)
    x_tiles = x_all.reshape(col_count, cb, block_edge, feat_dev)
    agg_f32 = jnp.einsum("trcij,tcjf->rif", dense, x_tiles, preferred_element_type=jnp.float32)
    aggregated = agg_f32.reshape(node_rows, feat_dev).astype(jnp.bfloat16)

    agg_parts = gather_rows(aggregated, "col", col_count).reshape(col_count, node_rows, feat_dev)
    agg_full = jnp.moveaxis(agg_parts, 0, 1).reshape(node_rows, col_count * feat_dev)
    own_pair = jnp.concatenate([features, grad_out], axis=0)
    pair_parts = gather_rows(own_pair, "col", col_count).reshape(col_count, 2, node_rows, feat_dev)
    pair_full = jnp.moveaxis(pair_parts, 0, 2).reshape(2, node_rows, col_count * feat_dev)
    feat_full = pair_full[0]
    grad_full = pair_full[1]
    preact = jnp.dot(agg_full, weight, preferred_element_type=jnp.float32) + jnp.dot(
        feat_full, root_weight, preferred_element_type=jnp.float32
    )
    preact_own = lax.dynamic_slice_in_dim(preact, col_index * feat_dev, feat_dev, 1)
    activations = jax.nn.silu(preact_own).astype(jnp.bfloat16)
    preact_grad = (grad_full.astype(jnp.float32) * silu_grad(preact)).astype(jnp.bfloat16)

    contract_rows = (((0,), (0,)), ((), ()))
    weight_part = lax.dot_general(
        aggregated, preact_grad, contract_rows, preferred_element_type=jnp.float32
    )
    root_part = lax.dot_general(
        features, preact_grad, contract_rows, preferred_element_type=jnp.float32
    )
    both = jnp.concatenate([weight_part, root_part], axis=0)
    both_sum = reduce_rows(both, "row", row_count)
    both_all = lax.all_gather(both_sum, "row", axis=0, tiled=True)
    nodes = row_count * node_rows
    grad_scale = 1.0 / math.sqrt(nodes)
    weight_sum = both_all[:feat_dev]
    root_sum = both_all[feat_dev:]

    w_rows = lax.dynamic_slice_in_dim(weight, col_index * feat_dev, feat_dev, 0)
    r_rows = lax.dynamic_slice_in_dim(root_weight, col_index * feat_dev, feat_dev, 0)
    contract_cols = (((1,), (1,)), ((), ()))
    aggregated_grad = lax.dot_general(
        preact_grad, w_rows, contract_cols, preferred_element_type=jnp.float32
    ).astype(jnp.bfloat16)
    own_grad = lax.dot_general(
        preact_grad, r_rows, contract_cols, preferred_element_type=jnp.float32
    )
    g_rows = aggregated_grad.reshape(row_blocks, block_edge, feat_dev)
    column_terms = jnp.einsum(
        "trcij,rif->tcjf", dense, g_rows, preferred_element_type=jnp.float32
    ).reshape(nodes, feat_dev)
    summed_cols = reduce_rows(column_terms.astype(jnp.bfloat16), "row", row_count)
    feature_grad = summed_cols + own_grad
    return (activations, feature_grad, weight_sum * grad_scale, root_sum * grad_scale)


def solution(mesh):
    in_specs = (
        P("row", "col"),
        P("row", "col"),
        P(),
        P(),
        P("row", "col", None, None, None),
        P("row", "col", None),
        P("row", "col"),
    )
    out_specs = (P("row", "col"), P("row", "col"), P("col", None), P("col", None))
    return jax.shard_map(
        per_device, mesh=mesh, in_specs=in_specs, out_specs=out_specs, check_vma=False
    )
```

```python
import math

import jax
import jax.numpy as jnp
from jax import lax
from jax.sharding import PartitionSpec as P


def silu_grad(preact):
    sig = jax.nn.sigmoid(preact)
    return sig * (1.0 + preact * (1.0 - sig))


def gather_rows(block, axis_name, parts):
    spread = jnp.broadcast_to(block[None], (parts,) + block.shape)
    got = lax.all_to_all(spread, axis_name, 0, 0, tiled=True)
    return got.reshape((parts * block.shape[0],) + block.shape[1:])


def reduce_rows(block, axis_name, parts):
    pieces = block.reshape((parts, block.shape[0] // parts) + block.shape[1:])
    got = lax.all_to_all(pieces, axis_name, 0, 0, tiled=True)
    return got.astype(jnp.float32).sum(0)


def per_device(features, grad_out, weight, root_weight, values, positions, counts):
    node_rows, feat_dev = features.shape
    slots, block_edge = values.shape[2], values.shape[-1]
    row_blocks = node_rows // block_edge
    col_count = lax.axis_size("col")
    row_count = lax.axis_size("row")
    col_index = lax.axis_index("col")

    live = (jnp.arange(slots, dtype=jnp.int32) < counts[0, 0]).astype(values.dtype)
    own_vals = (values[0, 0] * live[:, None, None]).reshape(slots * block_edge, block_edge)
    pos_row = jnp.zeros((16, block_edge), values.dtype)
    pos_row = lax.dynamic_update_slice(
        pos_row, positions[0, 0].astype(values.dtype).reshape(1, slots), (0, 0)
    )
    packed = jnp.concatenate([own_vals, pos_row], axis=0)
    all_packed = lax.all_gather(packed, "col", axis=0, tiled=True).reshape(
        col_count, slots * block_edge + 16, block_edge
    )
    tile_vals = all_packed[:, : slots * block_edge].reshape(
        col_count, slots, block_edge, block_edge
    )
    tile_pos = all_packed[:, slots * block_edge, :slots].astype(jnp.int32)
    cb = row_count * node_rows // col_count // block_edge
    n_pos = row_blocks * cb
    onehot = (tile_pos[:, :, None] == jnp.arange(n_pos, dtype=jnp.int32)[None, None, :]).astype(
        values.dtype
    )
    dense = jnp.einsum(
        "tsp,tsij->tpij", onehot, tile_vals, preferred_element_type=jnp.float32
    ).astype(values.dtype)
    dense = dense.reshape(col_count, row_blocks, cb, block_edge, block_edge)

    x_all = gather_rows(features, "row", row_count)
    x_tiles = x_all.reshape(col_count, cb, block_edge, feat_dev)
    agg_f32 = jnp.einsum("trcij,tcjf->rif", dense, x_tiles, preferred_element_type=jnp.float32)
    aggregated = agg_f32.reshape(node_rows, feat_dev).astype(jnp.bfloat16)

    agg_parts = gather_rows(aggregated, "col", col_count).reshape(col_count, node_rows, feat_dev)
    agg_full = jnp.moveaxis(agg_parts, 0, 1).reshape(node_rows, col_count * feat_dev)
    own_pair = jnp.concatenate([features, grad_out], axis=0)
    pair_parts = lax.all_gather(own_pair, "col", axis=0, tiled=True).reshape(
        col_count, 2, node_rows, feat_dev
    )
    pair_full = jnp.moveaxis(pair_parts, 0, 2).reshape(2, node_rows, col_count * feat_dev)
    feat_full = pair_full[0]
    grad_full = pair_full[1]
    preact = jnp.dot(agg_full, weight, preferred_element_type=jnp.float32) + jnp.dot(
        feat_full, root_weight, preferred_element_type=jnp.float32
    )
    preact_own = lax.dynamic_slice_in_dim(preact, col_index * feat_dev, feat_dev, 1)
    activations = jax.nn.silu(preact_own).astype(jnp.bfloat16)
    preact_grad = (grad_full.astype(jnp.float32) * silu_grad(preact)).astype(jnp.bfloat16)

    contract_rows = (((0,), (0,)), ((), ()))
    weight_part = lax.dot_general(
        aggregated, preact_grad, contract_rows, preferred_element_type=jnp.float32
    )
    root_part = lax.dot_general(
        features, preact_grad, contract_rows, preferred_element_type=jnp.float32
    )
    both = jnp.concatenate([weight_part, root_part], axis=0)
    both_sum = reduce_rows(both, "row", row_count)
    sum_high = both_sum.astype(jnp.bfloat16)
    sum_low = (both_sum - sum_high.astype(jnp.float32)).astype(jnp.bfloat16)
    sum_lanes = both_sum.size // block_edge
    sum_pair = jnp.concatenate(
        [sum_high.reshape(sum_lanes, block_edge), sum_low.reshape(sum_lanes, block_edge)], axis=0
    )
    nodes = row_count * node_rows
    grad_scale = 1.0 / math.sqrt(nodes)

    w_rows = lax.dynamic_slice_in_dim(weight, col_index * feat_dev, feat_dev, 0)
    r_rows = lax.dynamic_slice_in_dim(root_weight, col_index * feat_dev, feat_dev, 0)
    contract_cols = (((1,), (1,)), ((), ()))
    aggregated_grad = lax.dot_general(
        preact_grad, w_rows, contract_cols, preferred_element_type=jnp.float32
    ).astype(jnp.bfloat16)
    own_grad = lax.dot_general(
        preact_grad, r_rows, contract_cols, preferred_element_type=jnp.float32
    )
    g_rows = aggregated_grad.reshape(row_blocks, block_edge, feat_dev)
    column_terms = jnp.einsum(
        "trcij,rif->tcjf", dense, g_rows, preferred_element_type=jnp.float32
    ).reshape(nodes, feat_dev)
    term_pieces = column_terms.astype(jnp.bfloat16).reshape(row_count, node_rows, feat_dev)
    outgoing = jnp.concatenate(
        [term_pieces, jnp.broadcast_to(sum_pair[None], (row_count,) + sum_pair.shape)], axis=1
    )
    incoming = lax.all_to_all(outgoing, "row", 0, 0, tiled=True)
    summed_cols = incoming[:, :node_rows].astype(jnp.float32).sum(0)
    got_high = incoming[:, node_rows : node_rows + sum_lanes].astype(jnp.float32)
    got_low = incoming[:, node_rows + sum_lanes :].astype(jnp.float32)
    both_all = (got_high + got_low).reshape(both.shape)
    weight_sum = both_all[:feat_dev]
    root_sum = both_all[feat_dev:]
    feature_grad = summed_cols + own_grad
    return (activations, feature_grad, weight_sum * grad_scale, root_sum * grad_scale)


def solution(mesh):
    in_specs = (
        P("row", "col"),
        P("row", "col"),
        P(),
        P(),
        P("row", "col", None, None, None),
        P("row", "col", None),
        P("row", "col"),
    )
    out_specs = (P("row", "col"), P("row", "col"), P("col", None), P("col", None))
    return jax.shard_map(
        per_device, mesh=mesh, in_specs=in_specs, out_specs=out_specs, check_vma=False
    )
```

```python
import math

import jax
import jax.numpy as jnp
from jax import lax
from jax.sharding import PartitionSpec as P


def silu_grad(preact):
    sig = jax.nn.sigmoid(preact)
    return sig * (1.0 + preact * (1.0 - sig))


def gather_rows(block, axis_name, parts):
    spread = jnp.broadcast_to(block[None], (parts,) + block.shape)
    got = lax.all_to_all(spread, axis_name, 0, 0, tiled=True)
    return got.reshape((parts * block.shape[0],) + block.shape[1:])


def reduce_rows(block, axis_name, parts):
    pieces = block.reshape((parts, block.shape[0] // parts) + block.shape[1:])
    got = lax.all_to_all(pieces, axis_name, 0, 0, tiled=True)
    return got.astype(jnp.float32).sum(0)


def per_device(features, grad_out, weight, root_weight, values, positions, counts):
    node_rows, feat_dev = features.shape
    slots, block_edge = values.shape[2], values.shape[-1]
    row_blocks = node_rows // block_edge
    col_count = lax.axis_size("col")
    row_count = lax.axis_size("row")
    col_index = lax.axis_index("col")

    live = (jnp.arange(slots, dtype=jnp.int32) < counts[0, 0]).astype(values.dtype)
    own_vals = (values[0, 0] * live[:, None, None]).reshape(slots * block_edge, block_edge)
    pos_row = jnp.zeros((16, block_edge), values.dtype)
    pos_row = lax.dynamic_update_slice(
        pos_row, positions[0, 0].astype(values.dtype).reshape(1, slots), (0, 0)
    )
    packed = jnp.concatenate([own_vals, pos_row], axis=0)
    all_packed = lax.all_gather(packed, "col", axis=0, tiled=True).reshape(
        col_count, slots * block_edge + 16, block_edge
    )
    tile_vals = all_packed[:, : slots * block_edge].reshape(
        col_count, slots, block_edge, block_edge
    )
    tile_pos = all_packed[:, slots * block_edge, :slots].astype(jnp.int32)
    cb = row_count * node_rows // col_count // block_edge
    n_pos = row_blocks * cb
    onehot = (tile_pos[:, :, None] == jnp.arange(n_pos, dtype=jnp.int32)[None, None, :]).astype(
        values.dtype
    )
    dense = jnp.einsum(
        "tsp,tsij->tpij", onehot, tile_vals, preferred_element_type=jnp.float32
    ).astype(values.dtype)
    dense = dense.reshape(col_count, row_blocks, cb, block_edge, block_edge)

    x_all = gather_rows(features, "row", row_count)
    x_tiles = x_all.reshape(col_count, cb, block_edge, feat_dev)
    agg_f32 = jnp.einsum("trcij,tcjf->rif", dense, x_tiles, preferred_element_type=jnp.float32)
    aggregated = agg_f32.reshape(node_rows, feat_dev).astype(jnp.bfloat16)

    agg_parts = gather_rows(aggregated, "col", col_count).reshape(col_count, node_rows, feat_dev)
    agg_full = jnp.moveaxis(agg_parts, 0, 1).reshape(node_rows, col_count * feat_dev)
    own_pair = jnp.concatenate([features, grad_out], axis=0)
    pair_parts = lax.all_gather(own_pair, "col", axis=0, tiled=True).reshape(
        col_count, 2, node_rows, feat_dev
    )
    pair_full = jnp.moveaxis(pair_parts, 0, 2).reshape(2, node_rows, col_count * feat_dev)
    feat_full = pair_full[0]
    grad_full = pair_full[1]
    preact = jnp.dot(agg_full, weight, preferred_element_type=jnp.float32) + jnp.dot(
        feat_full, root_weight, preferred_element_type=jnp.float32
    )
    preact_own = lax.dynamic_slice_in_dim(preact, col_index * feat_dev, feat_dev, 1)
    activations = jax.nn.silu(preact_own).astype(jnp.bfloat16)
    preact_grad = (grad_full.astype(jnp.float32) * silu_grad(preact)).astype(jnp.bfloat16)

    contract_rows = (((0,), (0,)), ((), ()))
    weight_part = lax.dot_general(
        aggregated, preact_grad, contract_rows, preferred_element_type=jnp.float32
    )
    root_part = lax.dot_general(
        features, preact_grad, contract_rows, preferred_element_type=jnp.float32
    )
    nodes = row_count * node_rows
    grad_scale = 1.0 / math.sqrt(nodes)
    both = jnp.concatenate([weight_part, root_part], axis=0) * grad_scale
    both_sum = reduce_rows(both, "row", row_count)
    high_f32 = lax.reduce_precision(both_sum, exponent_bits=8, mantissa_bits=7)
    sum_high = high_f32.astype(jnp.bfloat16)
    sum_low = (both_sum - high_f32).astype(jnp.bfloat16)
    sum_lanes = both_sum.size // block_edge
    sum_pair = jnp.concatenate(
        [sum_high.reshape(sum_lanes, block_edge), sum_low.reshape(sum_lanes, block_edge)], axis=0
    )

    w_rows = lax.dynamic_slice_in_dim(weight, col_index * feat_dev, feat_dev, 0)
    r_rows = lax.dynamic_slice_in_dim(root_weight, col_index * feat_dev, feat_dev, 0)
    contract_cols = (((1,), (1,)), ((), ()))
    aggregated_grad = lax.dot_general(
        preact_grad, w_rows, contract_cols, preferred_element_type=jnp.float32
    ).astype(jnp.bfloat16)
    own_grad = lax.dot_general(
        preact_grad, r_rows, contract_cols, preferred_element_type=jnp.float32
    )
    g_rows = aggregated_grad.reshape(row_blocks, block_edge, feat_dev)
    column_terms = jnp.einsum(
        "trcij,rif->tcjf", dense, g_rows, preferred_element_type=jnp.float32
    ).reshape(nodes, feat_dev)
    term_pieces = column_terms.astype(jnp.bfloat16).reshape(row_count, node_rows, feat_dev)
    outgoing = jnp.concatenate(
        [term_pieces, jnp.broadcast_to(sum_pair[None], (row_count,) + sum_pair.shape)], axis=1
    )
    outgoing, own_grad = lax.optimization_barrier((outgoing, own_grad))
    incoming = lax.all_to_all(outgoing, "row", 0, 0, tiled=True)
    summed_cols = incoming[:, :node_rows].astype(jnp.float32).sum(0)
    got_high = incoming[:, node_rows : node_rows + sum_lanes].astype(jnp.float32)
    got_low = incoming[:, node_rows + sum_lanes :].astype(jnp.float32)
    both_all = (got_high + got_low).reshape(both.shape)
    weight_sum = both_all[:feat_dev]
    root_sum = both_all[feat_dev:]
    feature_grad = summed_cols + own_grad
    return (activations, feature_grad, weight_sum, root_sum)


def solution(mesh):
    in_specs = (
        P("row", "col"),
        P("row", "col"),
        P(),
        P(),
        P("row", "col", None, None, None),
        P("row", "col", None),
        P("row", "col"),
    )
    out_specs = (P("row", "col"), P("row", "col"), P("col", None), P("col", None))
    return jax.shard_map(
        per_device, mesh=mesh, in_specs=in_specs, out_specs=out_specs, check_vma=False
    )
```

```python
import math

import jax
import jax.numpy as jnp
from jax import lax
from jax.sharding import PartitionSpec as P


def silu_grad(preact):
    sig = jax.nn.sigmoid(preact)
    return sig * (1.0 + preact * (1.0 - sig))


def gather_rows(block, axis_name, parts):
    spread = jnp.broadcast_to(block[None], (parts,) + block.shape)
    got = lax.all_to_all(spread, axis_name, 0, 0, tiled=True)
    return got.reshape((parts * block.shape[0],) + block.shape[1:])


def reduce_rows(block, axis_name, parts):
    pieces = block.reshape((parts, block.shape[0] // parts) + block.shape[1:])
    got = lax.all_to_all(pieces, axis_name, 0, 0, tiled=True)
    return got.astype(jnp.float32).sum(0)


def per_device(features, grad_out, weight, root_weight, values, positions, counts):
    node_rows, feat_dev = features.shape
    slots, block_edge = values.shape[2], values.shape[-1]
    row_blocks = node_rows // block_edge
    col_count = lax.axis_size("col")
    row_count = lax.axis_size("row")
    col_index = lax.axis_index("col")

    live = (jnp.arange(slots, dtype=jnp.int32) < counts[0, 0]).astype(values.dtype)
    own_vals = (values[0, 0] * live[:, None, None]).reshape(slots * block_edge, block_edge)
    pos_row = jnp.zeros((16, block_edge), values.dtype)
    pos_row = lax.dynamic_update_slice(
        pos_row, positions[0, 0].astype(values.dtype).reshape(1, slots), (0, 0)
    )
    packed = jnp.concatenate([own_vals, pos_row], axis=0)
    all_packed = lax.all_gather(packed, "col", axis=0, tiled=True).reshape(
        col_count, slots * block_edge + 16, block_edge
    )
    tile_vals = all_packed[:, : slots * block_edge].reshape(
        col_count, slots, block_edge, block_edge
    )
    tile_pos = all_packed[:, slots * block_edge, :slots].astype(jnp.int32)
    cb = row_count * node_rows // col_count // block_edge
    n_pos = row_blocks * cb
    onehot = (tile_pos[:, :, None] == jnp.arange(n_pos, dtype=jnp.int32)[None, None, :]).astype(
        values.dtype
    )
    dense = jnp.einsum(
        "tsp,tsij->tpij", onehot, tile_vals, preferred_element_type=jnp.float32
    ).astype(values.dtype)
    dense = dense.reshape(col_count, row_blocks, cb, block_edge, block_edge)

    x_all = gather_rows(features, "row", row_count)
    x_tiles = x_all.reshape(col_count, cb, block_edge, feat_dev)
    agg_f32 = jnp.einsum("trcij,tcjf->rif", dense, x_tiles, preferred_element_type=jnp.float32)
    aggregated = agg_f32.reshape(node_rows, feat_dev).astype(jnp.bfloat16)

    agg_parts = gather_rows(aggregated, "col", col_count).reshape(col_count, node_rows, feat_dev)
    agg_full = jnp.moveaxis(agg_parts, 0, 1).reshape(node_rows, col_count * feat_dev)
    own_pair = jnp.concatenate([features, grad_out], axis=0)
    shifted = [own_pair] + [
        lax.ppermute(own_pair, "col", [(i, (i + k) % col_count) for i in range(col_count)])
        for k in range(1, col_count)
    ]
    by_source = (col_index - jnp.arange(col_count, dtype=jnp.int32)) % col_count
    pair_parts = jnp.stack(shifted)[by_source].reshape(col_count, 2, node_rows, feat_dev)
    pair_full = jnp.moveaxis(pair_parts, 0, 2).reshape(2, node_rows, col_count * feat_dev)
    feat_full = pair_full[0]
    grad_full = pair_full[1]
    preact = jnp.dot(agg_full, weight, preferred_element_type=jnp.float32) + jnp.dot(
        feat_full, root_weight, preferred_element_type=jnp.float32
    )
    preact_own = lax.dynamic_slice_in_dim(preact, col_index * feat_dev, feat_dev, 1)
    activations = jax.nn.silu(preact_own).astype(jnp.bfloat16)
    preact_grad = (grad_full.astype(jnp.float32) * silu_grad(preact)).astype(jnp.bfloat16)

    contract_rows = (((0,), (0,)), ((), ()))
    weight_part = lax.dot_general(
        aggregated, preact_grad, contract_rows, preferred_element_type=jnp.float32
    )
    root_part = lax.dot_general(
        features, preact_grad, contract_rows, preferred_element_type=jnp.float32
    )
    nodes = row_count * node_rows
    grad_scale = 1.0 / math.sqrt(nodes)
    both = jnp.concatenate([weight_part, root_part], axis=0) * grad_scale
    both_sum = reduce_rows(both, "row", row_count)
    high_f32 = lax.reduce_precision(both_sum, exponent_bits=8, mantissa_bits=7)
    sum_high = high_f32.astype(jnp.bfloat16)
    sum_low = (both_sum - high_f32).astype(jnp.bfloat16)
    sum_lanes = both_sum.size // block_edge
    sum_pair = jnp.concatenate(
        [sum_high.reshape(sum_lanes, block_edge), sum_low.reshape(sum_lanes, block_edge)], axis=0
    )

    w_rows = lax.dynamic_slice_in_dim(weight, col_index * feat_dev, feat_dev, 0)
    r_rows = lax.dynamic_slice_in_dim(root_weight, col_index * feat_dev, feat_dev, 0)
    contract_cols = (((1,), (1,)), ((), ()))
    aggregated_grad = lax.dot_general(
        preact_grad, w_rows, contract_cols, preferred_element_type=jnp.float32
    ).astype(jnp.bfloat16)
    own_grad = lax.dot_general(
        preact_grad, r_rows, contract_cols, preferred_element_type=jnp.float32
    )
    g_rows = aggregated_grad.reshape(row_blocks, block_edge, feat_dev)
    column_terms = jnp.einsum(
        "trcij,rif->tcjf", dense, g_rows, preferred_element_type=jnp.float32
    ).reshape(nodes, feat_dev)
    term_pieces = column_terms.astype(jnp.bfloat16).reshape(row_count, node_rows, feat_dev)
    outgoing = jnp.concatenate(
        [term_pieces, jnp.broadcast_to(sum_pair[None], (row_count,) + sum_pair.shape)], axis=1
    )
    outgoing, own_grad = lax.optimization_barrier((outgoing, own_grad))
    incoming = lax.all_to_all(outgoing, "row", 0, 0, tiled=True)
    summed_cols = incoming[:, :node_rows].astype(jnp.float32).sum(0)
    got_high = incoming[:, node_rows : node_rows + sum_lanes].astype(jnp.float32)
    got_low = incoming[:, node_rows + sum_lanes :].astype(jnp.float32)
    both_all = (got_high + got_low).reshape(both.shape)
    weight_sum = both_all[:feat_dev]
    root_sum = both_all[feat_dev:]
    feature_grad = summed_cols + own_grad
    return (activations, feature_grad, weight_sum, root_sum)


def solution(mesh):
    in_specs = (
        P("row", "col"),
        P("row", "col"),
        P(),
        P(),
        P("row", "col", None, None, None),
        P("row", "col", None),
        P("row", "col"),
    )
    out_specs = (P("row", "col"), P("row", "col"), P("col", None), P("col", None))
    return jax.shard_map(
        per_device, mesh=mesh, in_specs=in_specs, out_specs=out_specs, check_vma=False
    )
```

```python
import math

import jax
import jax.numpy as jnp
from jax import lax
from jax.sharding import PartitionSpec as P


def silu_grad(preact):
    sig = jax.nn.sigmoid(preact)
    return sig * (1.0 + preact * (1.0 - sig))


def gather_rows(block, axis_name, parts):
    spread = jnp.broadcast_to(block[None], (parts,) + block.shape)
    got = lax.all_to_all(spread, axis_name, 0, 0, tiled=True)
    return got.reshape((parts * block.shape[0],) + block.shape[1:])


def reduce_rows(block, axis_name, parts):
    pieces = block.reshape((parts, block.shape[0] // parts) + block.shape[1:])
    got = lax.all_to_all(pieces, axis_name, 0, 0, tiled=True)
    return got.astype(jnp.float32).sum(0)


def per_device(features, grad_out, weight, root_weight, values, positions, counts):
    node_rows, feat_dev = features.shape
    slots, block_edge = values.shape[2], values.shape[-1]
    row_blocks = node_rows // block_edge
    col_count = lax.axis_size("col")
    row_count = lax.axis_size("row")
    col_index = lax.axis_index("col")

    live = (jnp.arange(slots, dtype=jnp.int32) < counts[0, 0]).astype(values.dtype)
    own_vals = (values[0, 0] * live[:, None, None]).reshape(slots * block_edge, block_edge)
    pos_row = jnp.zeros((16, block_edge), values.dtype)
    pos_row = lax.dynamic_update_slice(
        pos_row, positions[0, 0].astype(values.dtype).reshape(1, slots), (0, 0)
    )
    packed = jnp.concatenate([own_vals, pos_row], axis=0)
    all_packed = lax.all_gather(packed, "col", axis=0, tiled=True).reshape(
        col_count, slots * block_edge + 16, block_edge
    )
    tile_vals = all_packed[:, : slots * block_edge].reshape(
        col_count, slots, block_edge, block_edge
    )
    tile_pos = all_packed[:, slots * block_edge, :slots].astype(jnp.int32)
    cb = row_count * node_rows // col_count // block_edge
    n_pos = row_blocks * cb
    onehot = (tile_pos[:, :, None] == jnp.arange(n_pos, dtype=jnp.int32)[None, None, :]).astype(
        values.dtype
    )
    dense = jnp.einsum(
        "tsp,tsij->tpij", onehot, tile_vals, preferred_element_type=jnp.float32
    ).astype(values.dtype)
    dense = dense.reshape(col_count, row_blocks, cb, block_edge, block_edge)

    x_all = gather_rows(features, "row", row_count)
    x_tiles = x_all.reshape(col_count, cb, block_edge, feat_dev)
    agg_f32 = jnp.einsum("trcij,tcjf->rif", dense, x_tiles, preferred_element_type=jnp.float32)
    aggregated = agg_f32.reshape(node_rows, feat_dev).astype(jnp.bfloat16)

    agg_parts = gather_rows(aggregated, "col", col_count).reshape(col_count, node_rows, feat_dev)
    agg_full = jnp.moveaxis(agg_parts, 0, 1).reshape(node_rows, col_count * feat_dev)
    own_pair = jnp.concatenate([features, grad_out], axis=0)
    pair_parts = lax.all_gather(own_pair, "col", axis=0, tiled=True).reshape(
        col_count, 2, node_rows, feat_dev
    )
    pair_full = jnp.moveaxis(pair_parts, 0, 2).reshape(2, node_rows, col_count * feat_dev)
    feat_full = pair_full[0]
    grad_full = pair_full[1]
    preact = jnp.dot(agg_full, weight, preferred_element_type=jnp.float32) + jnp.dot(
        feat_full, root_weight, preferred_element_type=jnp.float32
    )
    preact_own = lax.dynamic_slice_in_dim(preact, col_index * feat_dev, feat_dev, 1)
    activations = jax.nn.silu(preact_own).astype(jnp.bfloat16)
    preact_grad = (grad_full.astype(jnp.float32) * silu_grad(preact)).astype(jnp.bfloat16)

    contract_rows = (((0,), (0,)), ((), ()))
    weight_part = lax.dot_general(
        aggregated, preact_grad, contract_rows, preferred_element_type=jnp.float32
    )
    root_part = lax.dot_general(
        features, preact_grad, contract_rows, preferred_element_type=jnp.float32
    )
    nodes = row_count * node_rows
    grad_scale = 1.0 / math.sqrt(nodes)
    both = jnp.concatenate([weight_part, root_part], axis=0) * grad_scale
    both_sum = reduce_rows(both, "row", row_count)
    high_f32 = lax.reduce_precision(both_sum, exponent_bits=8, mantissa_bits=7)
    sum_high = high_f32.astype(jnp.bfloat16)
    sum_low = (both_sum - high_f32).astype(jnp.bfloat16)
    sum_lanes = both_sum.size // block_edge
    sum_pair = jnp.concatenate(
        [sum_high.reshape(sum_lanes, block_edge), sum_low.reshape(sum_lanes, block_edge)], axis=0
    )

    w_rows = lax.dynamic_slice_in_dim(weight, col_index * feat_dev, feat_dev, 0)
    r_rows = lax.dynamic_slice_in_dim(root_weight, col_index * feat_dev, feat_dev, 0)
    contract_cols = (((1,), (1,)), ((), ()))
    aggregated_grad = lax.dot_general(
        preact_grad, w_rows, contract_cols, preferred_element_type=jnp.float32
    ).astype(jnp.bfloat16)
    own_grad = lax.dot_general(
        preact_grad, r_rows, contract_cols, preferred_element_type=jnp.float32
    )
    g_rows = aggregated_grad.reshape(row_blocks, block_edge, feat_dev)
    column_terms = jnp.einsum(
        "trcij,rif->tcjf", dense, g_rows, preferred_element_type=jnp.float32
    ).reshape(nodes, feat_dev)
    term_pieces = column_terms.astype(jnp.bfloat16).reshape(row_count, node_rows, feat_dev)
    room = jnp.zeros((row_count,) + sum_pair.shape, term_pieces.dtype)
    outgoing = jnp.concatenate([term_pieces, room], axis=1)
    outgoing, own_grad = lax.optimization_barrier((outgoing, own_grad))
    outgoing = lax.dynamic_update_slice(
        outgoing, jnp.broadcast_to(sum_pair[None], room.shape), (0, node_rows, 0)
    )
    incoming = lax.all_to_all(outgoing, "row", 0, 0, tiled=True)
    summed_cols = incoming[:, :node_rows].astype(jnp.float32).sum(0)
    got_high = incoming[:, node_rows : node_rows + sum_lanes].astype(jnp.float32)
    got_low = incoming[:, node_rows + sum_lanes :].astype(jnp.float32)
    half = row_count // 2
    weight_sum = (got_high[:half] + got_low[:half]).reshape(feat_dev, -1)
    root_sum = (got_high[half:] + got_low[half:]).reshape(feat_dev, -1)
    feature_grad = summed_cols + own_grad
    return (activations, feature_grad, weight_sum, root_sum)


def solution(mesh):
    in_specs = (
        P("row", "col"),
        P("row", "col"),
        P(),
        P(),
        P("row", "col", None, None, None),
        P("row", "col", None),
        P("row", "col"),
    )
    out_specs = (P("row", "col"), P("row", "col"), P("col", None), P("col", None))
    return jax.shard_map(
        per_device, mesh=mesh, in_specs=in_specs, out_specs=out_specs, check_vma=False
    )
```

```python
import math

import jax
import jax.numpy as jnp
from jax import lax
from jax.sharding import PartitionSpec as P


def silu_grad(preact):
    sig = jax.nn.sigmoid(preact)
    return sig * (1.0 + preact * (1.0 - sig))


def gather_rows(block, axis_name, parts):
    spread = jnp.broadcast_to(block[None], (parts,) + block.shape)
    got = lax.all_to_all(spread, axis_name, 0, 0, tiled=True)
    return got.reshape((parts * block.shape[0],) + block.shape[1:])


def reduce_rows(block, axis_name, parts):
    pieces = block.reshape((parts, block.shape[0] // parts) + block.shape[1:])
    got = lax.all_to_all(pieces, axis_name, 0, 0, tiled=True)
    return got.astype(jnp.float32).sum(0)


def per_device(features, grad_out, weight, root_weight, values, positions, counts):
    node_rows, feat_dev = features.shape
    slots, block_edge = values.shape[2], values.shape[-1]
    row_blocks = node_rows // block_edge
    col_count = lax.axis_size("col")
    row_count = lax.axis_size("row")
    col_index = lax.axis_index("col")

    live = (jnp.arange(slots, dtype=jnp.int32) < counts[0, 0]).astype(values.dtype)
    own_vals = (values[0, 0] * live[:, None, None]).reshape(slots * block_edge, block_edge)
    pos_row = jnp.zeros((16, block_edge), values.dtype)
    pos_row = lax.dynamic_update_slice(
        pos_row, positions[0, 0].astype(values.dtype).reshape(1, slots), (0, 0)
    )
    packed = jnp.concatenate([own_vals, pos_row, features, grad_out], axis=0)
    all_packed = lax.all_gather(packed, "col", axis=0, tiled=True).reshape(
        col_count, packed.shape[0], block_edge
    )
    tile_vals = all_packed[:, : slots * block_edge].reshape(
        col_count, slots, block_edge, block_edge
    )
    tile_pos = all_packed[:, slots * block_edge, :slots].astype(jnp.int32)
    cb = row_count * node_rows // col_count // block_edge
    n_pos = row_blocks * cb
    onehot = (tile_pos[:, :, None] == jnp.arange(n_pos, dtype=jnp.int32)[None, None, :]).astype(
        values.dtype
    )
    dense = jnp.einsum(
        "tsp,tsij->tpij", onehot, tile_vals, preferred_element_type=jnp.float32
    ).astype(values.dtype)
    dense = dense.reshape(col_count, row_blocks, cb, block_edge, block_edge)

    x_all = gather_rows(features, "row", row_count)
    x_tiles = x_all.reshape(col_count, cb, block_edge, feat_dev)
    agg_f32 = jnp.einsum("trcij,tcjf->rif", dense, x_tiles, preferred_element_type=jnp.float32)
    aggregated = agg_f32.reshape(node_rows, feat_dev).astype(jnp.bfloat16)

    agg_parts = gather_rows(aggregated, "col", col_count).reshape(col_count, node_rows, feat_dev)
    agg_full = jnp.moveaxis(agg_parts, 0, 1).reshape(node_rows, col_count * feat_dev)
    pair_parts = all_packed[:, slots * block_edge + 16 :].reshape(
        col_count, 2, node_rows, feat_dev
    )
    pair_full = jnp.moveaxis(pair_parts, 0, 2).reshape(2, node_rows, col_count * feat_dev)
    feat_full = pair_full[0]
    grad_full = pair_full[1]
    preact = jnp.dot(agg_full, weight, preferred_element_type=jnp.float32) + jnp.dot(
        feat_full, root_weight, preferred_element_type=jnp.float32
    )
    preact_own = lax.dynamic_slice_in_dim(preact, col_index * feat_dev, feat_dev, 1)
    activations = jax.nn.silu(preact_own).astype(jnp.bfloat16)
    preact_grad = (grad_full.astype(jnp.float32) * silu_grad(preact)).astype(jnp.bfloat16)

    contract_rows = (((0,), (0,)), ((), ()))
    weight_part = lax.dot_general(
        aggregated, preact_grad, contract_rows, preferred_element_type=jnp.float32
    )
    root_part = lax.dot_general(
        features, preact_grad, contract_rows, preferred_element_type=jnp.float32
    )
    nodes = row_count * node_rows
    grad_scale = 1.0 / math.sqrt(nodes)
    both = jnp.concatenate([weight_part, root_part], axis=0) * grad_scale
    both_sum = reduce_rows(both, "row", row_count)
    high_f32 = lax.reduce_precision(both_sum, exponent_bits=8, mantissa_bits=7)
    sum_high = high_f32.astype(jnp.bfloat16)
    sum_low = (both_sum - high_f32).astype(jnp.bfloat16)
    sum_lanes = both_sum.size // block_edge
    sum_pair = jnp.concatenate(
        [sum_high.reshape(sum_lanes, block_edge), sum_low.reshape(sum_lanes, block_edge)], axis=0
    )

    w_rows = lax.dynamic_slice_in_dim(weight, col_index * feat_dev, feat_dev, 0)
    r_rows = lax.dynamic_slice_in_dim(root_weight, col_index * feat_dev, feat_dev, 0)
    contract_cols = (((1,), (1,)), ((), ()))
    aggregated_grad = lax.dot_general(
        preact_grad, w_rows, contract_cols, preferred_element_type=jnp.float32
    ).astype(jnp.bfloat16)
    own_grad = lax.dot_general(
        preact_grad, r_rows, contract_cols, preferred_element_type=jnp.float32
    )
    g_rows = aggregated_grad.reshape(row_blocks, block_edge, feat_dev)
    column_terms = jnp.einsum(
        "trcij,rif->tcjf", dense, g_rows, preferred_element_type=jnp.float32
    ).reshape(nodes, feat_dev)
    term_pieces = column_terms.astype(jnp.bfloat16).reshape(row_count, node_rows, feat_dev)
    room = jnp.zeros((row_count,) + sum_pair.shape, term_pieces.dtype)
    outgoing = jnp.concatenate([term_pieces, room], axis=1)
    outgoing, own_grad = lax.optimization_barrier((outgoing, own_grad))
    outgoing = lax.dynamic_update_slice(
        outgoing, jnp.broadcast_to(sum_pair[None], room.shape), (0, node_rows, 0)
    )
    incoming = lax.all_to_all(outgoing, "row", 0, 0, tiled=True)
    summed_cols = incoming[:, :node_rows].astype(jnp.float32).sum(0)
    got_high = incoming[:, node_rows : node_rows + sum_lanes].astype(jnp.float32)
    got_low = incoming[:, node_rows + sum_lanes :].astype(jnp.float32)
    half = row_count // 2
    weight_sum = (got_high[:half] + got_low[:half]).reshape(feat_dev, -1)
    root_sum = (got_high[half:] + got_low[half:]).reshape(feat_dev, -1)
    feature_grad = summed_cols + own_grad
    return (activations, feature_grad, weight_sum, root_sum)


def solution(mesh):
    in_specs = (
        P("row", "col"),
        P("row", "col"),
        P(),
        P(),
        P("row", "col", None, None, None),
        P("row", "col", None),
        P("row", "col"),
    )
    out_specs = (P("row", "col"), P("row", "col"), P("col", None), P("col", None))
    return jax.shard_map(
        per_device, mesh=mesh, in_specs=in_specs, out_specs=out_specs, check_vma=False
    )
```

```python
import math

import jax
import jax.numpy as jnp
from jax import lax
from jax.sharding import PartitionSpec as P


def silu_grad(preact):
    sig = jax.nn.sigmoid(preact)
    return sig * (1.0 + preact * (1.0 - sig))


def gather_rows(block, axis_name, parts):
    spread = jnp.broadcast_to(block[None], (parts,) + block.shape)
    got = lax.all_to_all(spread, axis_name, 0, 0, tiled=True)
    return got.reshape((parts * block.shape[0],) + block.shape[1:])


def reduce_rows(block, axis_name, parts):
    pieces = block.reshape((parts, block.shape[0] // parts) + block.shape[1:])
    got = lax.all_to_all(pieces, axis_name, 0, 0, tiled=True)
    return got.astype(jnp.float32).sum(0)


def per_device(features, grad_out, weight, root_weight, values, positions, counts):
    node_rows, feat_dev = features.shape
    slots, block_edge = values.shape[2], values.shape[-1]
    row_blocks = node_rows // block_edge
    col_count = lax.axis_size("col")
    row_count = lax.axis_size("row")
    col_index = lax.axis_index("col")

    live = (jnp.arange(slots, dtype=jnp.int32) < counts[0, 0]).astype(values.dtype)
    own_vals = (values[0, 0] * live[:, None, None]).reshape(slots * block_edge, block_edge)
    pos_row = jnp.zeros((16, block_edge), values.dtype)
    pos_row = lax.dynamic_update_slice(
        pos_row, positions[0, 0].astype(values.dtype).reshape(1, slots), (0, 0)
    )
    packed = jnp.concatenate([own_vals, pos_row, features, grad_out], axis=0)
    all_packed = lax.all_gather(packed, "col", axis=0, tiled=True).reshape(
        col_count, packed.shape[0], block_edge
    )
    tile_vals = all_packed[:, : slots * block_edge].reshape(
        col_count, slots, block_edge, block_edge
    )
    tile_pos = all_packed[:, slots * block_edge, :slots].astype(jnp.int32)
    cb = row_count * node_rows // col_count // block_edge
    n_pos = row_blocks * cb
    onehot = (tile_pos[:, :, None] == jnp.arange(n_pos, dtype=jnp.int32)[None, None, :]).astype(
        values.dtype
    )
    dense = jnp.einsum(
        "tsp,tsij->tpij", onehot, tile_vals, preferred_element_type=jnp.float32
    ).astype(values.dtype)
    dense = dense.reshape(col_count, row_blocks, cb, block_edge, block_edge)

    x_all = gather_rows(features, "row", row_count)
    x_tiles = x_all.reshape(col_count, cb, block_edge, feat_dev)
    col_hot = (
        (tile_pos % cb)[:, :, None] == jnp.arange(cb, dtype=jnp.int32)[None, None, :]
    ).astype(values.dtype)
    row_hot = (
        (tile_pos // cb)[:, :, None] == jnp.arange(row_blocks, dtype=jnp.int32)[None, None, :]
    ).astype(jnp.float32)
    chosen = jnp.einsum(
        "tsc,tcjf->tsjf", col_hot, x_tiles, preferred_element_type=jnp.float32
    ).astype(values.dtype)
    products = jnp.einsum(
        "tsij,tsjf->tsif", tile_vals, chosen, preferred_element_type=jnp.float32
    )
    agg_f32 = jnp.einsum("tsr,tsif->rif", row_hot, products, precision=lax.Precision.HIGHEST)
    aggregated = agg_f32.reshape(node_rows, feat_dev).astype(jnp.bfloat16)

    agg_parts = gather_rows(aggregated, "col", col_count).reshape(col_count, node_rows, feat_dev)
    agg_full = jnp.moveaxis(agg_parts, 0, 1).reshape(node_rows, col_count * feat_dev)
    pair_parts = all_packed[:, slots * block_edge + 16 :].reshape(
        col_count, 2, node_rows, feat_dev
    )
    pair_full = jnp.moveaxis(pair_parts, 0, 2).reshape(2, node_rows, col_count * feat_dev)
    feat_full = pair_full[0]
    grad_full = pair_full[1]
    preact = jnp.dot(agg_full, weight, preferred_element_type=jnp.float32) + jnp.dot(
        feat_full, root_weight, preferred_element_type=jnp.float32
    )
    preact_own = lax.dynamic_slice_in_dim(preact, col_index * feat_dev, feat_dev, 1)
    activations = jax.nn.silu(preact_own).astype(jnp.bfloat16)
    preact_grad = (grad_full.astype(jnp.float32) * silu_grad(preact)).astype(jnp.bfloat16)

    contract_rows = (((0,), (0,)), ((), ()))
    weight_part = lax.dot_general(
        aggregated, preact_grad, contract_rows, preferred_element_type=jnp.float32
    )
    root_part = lax.dot_general(
        features, preact_grad, contract_rows, preferred_element_type=jnp.float32
    )
    nodes = row_count * node_rows
    grad_scale = 1.0 / math.sqrt(nodes)
    both = jnp.concatenate([weight_part, root_part], axis=0) * grad_scale
    both_sum = reduce_rows(both, "row", row_count)
    high_f32 = lax.reduce_precision(both_sum, exponent_bits=8, mantissa_bits=7)
    sum_high = high_f32.astype(jnp.bfloat16)
    sum_low = (both_sum - high_f32).astype(jnp.bfloat16)
    sum_lanes = both_sum.size // block_edge
    sum_pair = jnp.concatenate(
        [sum_high.reshape(sum_lanes, block_edge), sum_low.reshape(sum_lanes, block_edge)], axis=0
    )

    w_rows = lax.dynamic_slice_in_dim(weight, col_index * feat_dev, feat_dev, 0)
    r_rows = lax.dynamic_slice_in_dim(root_weight, col_index * feat_dev, feat_dev, 0)
    contract_cols = (((1,), (1,)), ((), ()))
    aggregated_grad = lax.dot_general(
        preact_grad, w_rows, contract_cols, preferred_element_type=jnp.float32
    ).astype(jnp.bfloat16)
    own_grad = lax.dot_general(
        preact_grad, r_rows, contract_cols, preferred_element_type=jnp.float32
    )
    g_rows = aggregated_grad.reshape(row_blocks, block_edge, feat_dev)
    column_terms = jnp.einsum(
        "trcij,rif->tcjf", dense, g_rows, preferred_element_type=jnp.float32
    ).reshape(nodes, feat_dev)
    term_pieces = column_terms.astype(jnp.bfloat16).reshape(row_count, node_rows, feat_dev)
    room = jnp.zeros((row_count,) + sum_pair.shape, term_pieces.dtype)
    outgoing = jnp.concatenate([term_pieces, room], axis=1)
    outgoing, own_grad = lax.optimization_barrier((outgoing, own_grad))
    outgoing = lax.dynamic_update_slice(
        outgoing, jnp.broadcast_to(sum_pair[None], room.shape), (0, node_rows, 0)
    )
    incoming = lax.all_to_all(outgoing, "row", 0, 0, tiled=True)
    summed_cols = incoming[:, :node_rows].astype(jnp.float32).sum(0)
    got_high = incoming[:, node_rows : node_rows + sum_lanes].astype(jnp.float32)
    got_low = incoming[:, node_rows + sum_lanes :].astype(jnp.float32)
    half = row_count // 2
    weight_sum = (got_high[:half] + got_low[:half]).reshape(feat_dev, -1)
    root_sum = (got_high[half:] + got_low[half:]).reshape(feat_dev, -1)
    feature_grad = summed_cols + own_grad
    return (activations, feature_grad, weight_sum, root_sum)


def solution(mesh):
    in_specs = (
        P("row", "col"),
        P("row", "col"),
        P(),
        P(),
        P("row", "col", None, None, None),
        P("row", "col", None),
        P("row", "col"),
    )
    out_specs = (P("row", "col"), P("row", "col"), P("col", None), P("col", None))
    return jax.shard_map(
        per_device, mesh=mesh, in_specs=in_specs, out_specs=out_specs, check_vma=False
    )
```

```python
import math

import jax
import jax.numpy as jnp
from jax import lax
from jax.sharding import PartitionSpec as P


def silu_grad(preact):
    sig = jax.nn.sigmoid(preact)
    return sig * (1.0 + preact * (1.0 - sig))


def gather_rows(block, axis_name, parts):
    spread = jnp.broadcast_to(block[None], (parts,) + block.shape)
    got = lax.all_to_all(spread, axis_name, 0, 0, tiled=True)
    return got.reshape((parts * block.shape[0],) + block.shape[1:])


def reduce_rows(block, axis_name, parts):
    pieces = block.reshape((parts, block.shape[0] // parts) + block.shape[1:])
    got = lax.all_to_all(pieces, axis_name, 0, 0, tiled=True)
    return got.astype(jnp.float32).sum(0)


def per_device(features, grad_out, weight, root_weight, values, positions, counts):
    node_rows, feat_dev = features.shape
    slots, block_edge = values.shape[2], values.shape[-1]
    row_blocks = node_rows // block_edge
    col_count = lax.axis_size("col")
    row_count = lax.axis_size("row")
    col_index = lax.axis_index("col")

    live = (jnp.arange(slots, dtype=jnp.int32) < counts[0, 0]).astype(values.dtype)
    own_vals = (values[0, 0] * live[:, None, None]).reshape(slots * block_edge, block_edge)
    pos_row = jnp.zeros((16, block_edge), values.dtype)
    pos_row = lax.dynamic_update_slice(
        pos_row, positions[0, 0].astype(values.dtype).reshape(1, slots), (0, 0)
    )
    packed = jnp.concatenate([own_vals, pos_row, features, grad_out], axis=0)
    all_packed = lax.all_gather(packed, "col", axis=0, tiled=True).reshape(
        col_count, packed.shape[0], block_edge
    )
    tile_vals = all_packed[:, : slots * block_edge].reshape(
        col_count, slots, block_edge, block_edge
    )
    tile_pos = all_packed[:, slots * block_edge, :slots].astype(jnp.int32)
    cb = row_count * node_rows // col_count // block_edge
    n_pos = row_blocks * cb
    onehot = (tile_pos[:, :, None] == jnp.arange(n_pos, dtype=jnp.int32)[None, None, :]).astype(
        values.dtype
    )
    dense = jnp.einsum(
        "tsp,tsij->tpij", onehot, tile_vals, preferred_element_type=jnp.float32
    ).astype(values.dtype)
    dense = dense.reshape(col_count, row_blocks, cb, block_edge, block_edge)

    x_all = gather_rows(features, "row", row_count)
    x_tiles = x_all.reshape(col_count, cb, block_edge, feat_dev)
    col_hot = (
        (tile_pos % cb)[:, :, None] == jnp.arange(cb, dtype=jnp.int32)[None, None, :]
    ).astype(values.dtype)
    row_hot = (
        (tile_pos // cb)[:, :, None] == jnp.arange(row_blocks, dtype=jnp.int32)[None, None, :]
    ).astype(jnp.float32)
    chosen = jnp.einsum(
        "tsc,tcjf->tsjf", col_hot, x_tiles, preferred_element_type=jnp.float32
    ).astype(values.dtype)
    products = jnp.einsum(
        "tsij,tsjf->tsif", tile_vals, chosen, preferred_element_type=jnp.float32
    )
    agg_f32 = jnp.einsum("tsr,tsif->rif", row_hot, products, precision=lax.Precision.HIGHEST)
    aggregated = agg_f32.reshape(node_rows, feat_dev).astype(jnp.bfloat16)

    agg_parts = gather_rows(aggregated, "col", col_count).reshape(col_count, node_rows, feat_dev)
    nodes = row_count * node_rows
    dense_t = jnp.transpose(dense, (0, 2, 4, 1, 3)).reshape(nodes, node_rows)
    agg_parts, dense_t = lax.optimization_barrier((agg_parts, dense_t))
    agg_full = jnp.moveaxis(agg_parts, 0, 1).reshape(node_rows, col_count * feat_dev)
    pair_parts = all_packed[:, slots * block_edge + 16 :].reshape(
        col_count, 2, node_rows, feat_dev
    )
    pair_full = jnp.moveaxis(pair_parts, 0, 2).reshape(2, node_rows, col_count * feat_dev)
    feat_full = pair_full[0]
    grad_full = pair_full[1]
    preact = jnp.dot(agg_full, weight, preferred_element_type=jnp.float32) + jnp.dot(
        feat_full, root_weight, preferred_element_type=jnp.float32
    )
    preact_own = lax.dynamic_slice_in_dim(preact, col_index * feat_dev, feat_dev, 1)
    activations = jax.nn.silu(preact_own).astype(jnp.bfloat16)
    preact_grad = (grad_full.astype(jnp.float32) * silu_grad(preact)).astype(jnp.bfloat16)

    contract_rows = (((0,), (0,)), ((), ()))
    weight_part = lax.dot_general(
        aggregated, preact_grad, contract_rows, preferred_element_type=jnp.float32
    )
    root_part = lax.dot_general(
        features, preact_grad, contract_rows, preferred_element_type=jnp.float32
    )
    grad_scale = 1.0 / math.sqrt(nodes)
    both = jnp.concatenate([weight_part, root_part], axis=0) * grad_scale
    both_sum = reduce_rows(both, "row", row_count)
    high_f32 = lax.reduce_precision(both_sum, exponent_bits=8, mantissa_bits=7)
    sum_high = high_f32.astype(jnp.bfloat16)
    sum_low = (both_sum - high_f32).astype(jnp.bfloat16)
    sum_lanes = both_sum.size // block_edge
    sum_pair = jnp.concatenate(
        [sum_high.reshape(sum_lanes, block_edge), sum_low.reshape(sum_lanes, block_edge)], axis=0
    )

    w_rows = lax.dynamic_slice_in_dim(weight, col_index * feat_dev, feat_dev, 0)
    r_rows = lax.dynamic_slice_in_dim(root_weight, col_index * feat_dev, feat_dev, 0)
    contract_cols = (((1,), (1,)), ((), ()))
    aggregated_grad = lax.dot_general(
        preact_grad, w_rows, contract_cols, preferred_element_type=jnp.float32
    ).astype(jnp.bfloat16)
    own_grad = lax.dot_general(
        preact_grad, r_rows, contract_cols, preferred_element_type=jnp.float32
    )
    column_terms = jnp.dot(dense_t, aggregated_grad, preferred_element_type=jnp.float32)
    term_pieces = column_terms.astype(jnp.bfloat16).reshape(row_count, node_rows, feat_dev)
    room = jnp.zeros((row_count,) + sum_pair.shape, term_pieces.dtype)
    outgoing = jnp.concatenate([term_pieces, room], axis=1)
    outgoing, own_grad = lax.optimization_barrier((outgoing, own_grad))
    outgoing = lax.dynamic_update_slice(
        outgoing, jnp.broadcast_to(sum_pair[None], room.shape), (0, node_rows, 0)
    )
    incoming = lax.all_to_all(outgoing, "row", 0, 0, tiled=True)
    summed_cols = incoming[:, :node_rows].astype(jnp.float32).sum(0)
    got_high = incoming[:, node_rows : node_rows + sum_lanes].astype(jnp.float32)
    got_low = incoming[:, node_rows + sum_lanes :].astype(jnp.float32)
    half = row_count // 2
    weight_sum = (got_high[:half] + got_low[:half]).reshape(feat_dev, -1)
    root_sum = (got_high[half:] + got_low[half:]).reshape(feat_dev, -1)
    feature_grad = summed_cols + own_grad
    return (activations, feature_grad, weight_sum, root_sum)


def solution(mesh):
    in_specs = (
        P("row", "col"),
        P("row", "col"),
        P(),
        P(),
        P("row", "col", None, None, None),
        P("row", "col", None),
        P("row", "col"),
    )
    out_specs = (P("row", "col"), P("row", "col"), P("col", None), P("col", None))
    return jax.shard_map(
        per_device, mesh=mesh, in_specs=in_specs, out_specs=out_specs, check_vma=False
    )
```

```python
import math

import jax
import jax.numpy as jnp
from jax import lax
from jax.sharding import PartitionSpec as P


def silu_grad(preact):
    sig = jax.nn.sigmoid(preact)
    return sig * (1.0 + preact * (1.0 - sig))


def gather_rows(block, axis_name, parts):
    spread = jnp.broadcast_to(block[None], (parts,) + block.shape)
    got = lax.all_to_all(spread, axis_name, 0, 0, tiled=True)
    return got.reshape((parts * block.shape[0],) + block.shape[1:])


def reduce_rows(block, axis_name, parts):
    pieces = block.reshape((parts, block.shape[0] // parts) + block.shape[1:])
    got = lax.all_to_all(pieces, axis_name, 0, 0, tiled=True)
    return got.astype(jnp.float32).sum(0)


def per_device(features, grad_out, weight, root_weight, values, positions, counts):
    node_rows, feat_dev = features.shape
    slots, block_edge = values.shape[2], values.shape[-1]
    row_blocks = node_rows // block_edge
    col_count = lax.axis_size("col")
    row_count = lax.axis_size("row")
    col_index = lax.axis_index("col")

    live = (jnp.arange(slots, dtype=jnp.int32) < counts[0, 0]).astype(values.dtype)
    own_vals = (values[0, 0] * live[:, None, None]).reshape(slots * block_edge, block_edge)
    pos_row = jnp.zeros((16, block_edge), values.dtype)
    pos_row = lax.dynamic_update_slice(
        pos_row, positions[0, 0].astype(values.dtype).reshape(1, slots), (0, 0)
    )
    packed = jnp.concatenate([own_vals, pos_row, features, grad_out], axis=0)
    all_packed = lax.all_gather(packed, "col", axis=0, tiled=True).reshape(
        col_count, packed.shape[0], block_edge
    )
    tile_vals = all_packed[:, : slots * block_edge].reshape(
        col_count, slots, block_edge, block_edge
    )
    tile_pos = all_packed[:, slots * block_edge, :slots].astype(jnp.int32)
    cb = row_count * node_rows // col_count // block_edge
    n_pos = row_blocks * cb
    onehot = (tile_pos[:, :, None] == jnp.arange(n_pos, dtype=jnp.int32)[None, None, :]).astype(
        values.dtype
    )
    dense = jnp.einsum(
        "tsp,tsij->tpij", onehot, tile_vals, preferred_element_type=jnp.float32
    ).astype(values.dtype)
    dense = dense.reshape(col_count, row_blocks, cb, block_edge, block_edge)

    x_all = gather_rows(features, "row", row_count)
    x_tiles = x_all.reshape(col_count, cb, block_edge, feat_dev)
    col_hot = (
        (tile_pos % cb)[:, :, None] == jnp.arange(cb, dtype=jnp.int32)[None, None, :]
    ).astype(values.dtype)
    row_hot = (
        (tile_pos // cb)[:, :, None] == jnp.arange(row_blocks, dtype=jnp.int32)[None, None, :]
    ).astype(jnp.float32)
    chosen = jnp.einsum(
        "tsc,tcjf->tsjf", col_hot, x_tiles, preferred_element_type=jnp.float32
    ).astype(values.dtype)
    products = jnp.einsum(
        "tsij,tsjf->tsif", tile_vals, chosen, preferred_element_type=jnp.float32
    )
    agg_f32 = jnp.einsum("tsr,tsif->rif", row_hot, products, precision=lax.Precision.HIGHEST)
    aggregated = agg_f32.reshape(node_rows, feat_dev).astype(jnp.bfloat16)

    agg_parts = gather_rows(aggregated, "col", col_count).reshape(col_count, node_rows, feat_dev)
    nodes = row_count * node_rows
    dense_t = jnp.transpose(dense, (0, 2, 4, 1, 3)).reshape(nodes, node_rows)
    agg_parts, dense_t = lax.optimization_barrier((agg_parts, dense_t))
    agg_full = jnp.moveaxis(agg_parts, 0, 1).reshape(node_rows, col_count * feat_dev)
    pair_parts = all_packed[:, slots * block_edge + 16 :].reshape(
        col_count, 2, node_rows, feat_dev
    )
    pair_full = jnp.moveaxis(pair_parts, 0, 2).reshape(2, node_rows, col_count * feat_dev)
    feat_full = pair_full[0]
    grad_full = pair_full[1]
    preact = jnp.dot(agg_full, weight, preferred_element_type=jnp.float32) + jnp.dot(
        feat_full, root_weight, preferred_element_type=jnp.float32
    )
    preact_own = lax.dynamic_slice_in_dim(preact, col_index * feat_dev, feat_dev, 1)
    activations = jax.nn.silu(preact_own).astype(jnp.bfloat16)
    preact_grad = (grad_full.astype(jnp.float32) * silu_grad(preact)).astype(jnp.bfloat16)

    contract_rows = (((0,), (0,)), ((), ()))
    weight_part = lax.dot_general(
        aggregated, preact_grad, contract_rows, preferred_element_type=jnp.float32
    )
    root_part = lax.dot_general(
        features, preact_grad, contract_rows, preferred_element_type=jnp.float32
    )
    grad_scale = 1.0 / math.sqrt(nodes)
    both = jnp.concatenate([weight_part, root_part], axis=0) * grad_scale
    both_sum = reduce_rows(both, "row", row_count)
    sum_lanes = both_sum.size // block_edge
    sum_pair = both_sum.astype(jnp.bfloat16).reshape(sum_lanes, block_edge)

    w_rows = lax.dynamic_slice_in_dim(weight, col_index * feat_dev, feat_dev, 0)
    r_rows = lax.dynamic_slice_in_dim(root_weight, col_index * feat_dev, feat_dev, 0)
    contract_cols = (((1,), (1,)), ((), ()))
    aggregated_grad = lax.dot_general(
        preact_grad, w_rows, contract_cols, preferred_element_type=jnp.float32
    ).astype(jnp.bfloat16)
    own_grad = lax.dot_general(
        preact_grad, r_rows, contract_cols, preferred_element_type=jnp.float32
    )
    column_terms = jnp.dot(dense_t, aggregated_grad, preferred_element_type=jnp.float32)
    term_pieces = column_terms.astype(jnp.bfloat16).reshape(row_count, node_rows, feat_dev)
    room = jnp.zeros((row_count,) + sum_pair.shape, term_pieces.dtype)
    outgoing = jnp.concatenate([term_pieces, room], axis=1)
    outgoing, own_grad = lax.optimization_barrier((outgoing, own_grad))
    outgoing = lax.dynamic_update_slice(
        outgoing, jnp.broadcast_to(sum_pair[None], room.shape), (0, node_rows, 0)
    )
    incoming = lax.all_to_all(outgoing, "row", 0, 0, tiled=True)
    summed_cols = incoming[:, :node_rows].astype(jnp.float32).sum(0)
    got_sums = incoming[:, node_rows:].astype(jnp.float32)
    half = row_count // 2
    weight_sum = got_sums[:half].reshape(feat_dev, -1)
    root_sum = got_sums[half:].reshape(feat_dev, -1)
    feature_grad = summed_cols + own_grad
    return (activations, feature_grad, weight_sum, root_sum)


def solution(mesh):
    in_specs = (
        P("row", "col"),
        P("row", "col"),
        P(),
        P(),
        P("row", "col", None, None, None),
        P("row", "col", None),
        P("row", "col"),
    )
    out_specs = (P("row", "col"), P("row", "col"), P("col", None), P("col", None))
    return jax.shard_map(
        per_device, mesh=mesh, in_specs=in_specs, out_specs=out_specs, check_vma=False
    )
```

```python
import math

import jax
import jax.numpy as jnp
from jax import lax
from jax.sharding import PartitionSpec as P


def silu_grad(preact):
    sig = jax.nn.sigmoid(preact)
    return sig * (1.0 + preact * (1.0 - sig))


def gather_rows(block, axis_name, parts):
    spread = jnp.broadcast_to(block[None], (parts,) + block.shape)
    got = lax.all_to_all(spread, axis_name, 0, 0, tiled=True)
    return got.reshape((parts * block.shape[0],) + block.shape[1:])


def reduce_rows(block, axis_name, parts):
    pieces = block.reshape((parts, block.shape[0] // parts) + block.shape[1:])
    got = lax.all_to_all(pieces, axis_name, 0, 0, tiled=True)
    return got.astype(jnp.float32).sum(0)


def per_device(features, grad_out, weight, root_weight, values, positions, counts):
    node_rows, feat_dev = features.shape
    slots, block_edge = values.shape[2], values.shape[-1]
    row_blocks = node_rows // block_edge
    col_count = lax.axis_size("col")
    row_count = lax.axis_size("row")
    col_index = lax.axis_index("col")

    live = (jnp.arange(slots, dtype=jnp.int32) < counts[0, 0]).astype(values.dtype)
    own_vals = (values[0, 0] * live[:, None, None]).reshape(slots * block_edge, block_edge)
    pos_row = jnp.zeros((16, block_edge), values.dtype)
    pos_row = lax.dynamic_update_slice(
        pos_row, positions[0, 0].astype(values.dtype).reshape(1, slots), (0, 0)
    )
    packed = jnp.concatenate([own_vals, pos_row, features, grad_out], axis=0)
    all_packed = lax.all_gather(packed, "col", axis=0, tiled=True).reshape(
        col_count, packed.shape[0], block_edge
    )
    tile_vals = all_packed[:, : slots * block_edge].reshape(
        col_count, slots, block_edge, block_edge
    )
    tile_pos = all_packed[:, slots * block_edge, :slots].astype(jnp.int32)
    cb = row_count * node_rows // col_count // block_edge
    n_pos = row_blocks * cb
    onehot = (tile_pos[:, :, None] == jnp.arange(n_pos, dtype=jnp.int32)[None, None, :]).astype(
        values.dtype
    )
    dense = jnp.einsum(
        "tsp,tsij->tpij", onehot, tile_vals, preferred_element_type=jnp.float32
    ).astype(values.dtype)
    dense = dense.reshape(col_count, row_blocks, cb, block_edge, block_edge)

    x_all = gather_rows(features, "row", row_count)
    x_tiles = x_all.reshape(col_count, cb, block_edge, feat_dev)
    col_hot = (
        (tile_pos % cb)[:, :, None] == jnp.arange(cb, dtype=jnp.int32)[None, None, :]
    ).astype(values.dtype)
    row_hot = (
        (tile_pos // cb)[:, :, None] == jnp.arange(row_blocks, dtype=jnp.int32)[None, None, :]
    ).astype(jnp.float32)
    chosen = jnp.einsum(
        "tsc,tcjf->tsjf", col_hot, x_tiles, preferred_element_type=jnp.float32
    ).astype(values.dtype)
    products = jnp.einsum(
        "tsij,tsjf->tsif", tile_vals, chosen, preferred_element_type=jnp.float32
    )
    agg_f32 = jnp.einsum("tsr,tsif->rif", row_hot, products, precision=lax.Precision.HIGHEST)
    aggregated = agg_f32.reshape(node_rows, feat_dev).astype(jnp.bfloat16)

    agg_parts = gather_rows(aggregated, "col", col_count).reshape(col_count, node_rows, feat_dev)
    nodes = row_count * node_rows
    dense_t = jnp.transpose(dense, (0, 2, 4, 1, 3)).reshape(nodes, node_rows)
    agg_parts, dense_t = lax.optimization_barrier((agg_parts, dense_t))
    agg_full = jnp.moveaxis(agg_parts, 0, 1).reshape(node_rows, col_count * feat_dev)
    pair_parts = all_packed[:, slots * block_edge + 16 :].reshape(
        col_count, 2, node_rows, feat_dev
    )
    pair_full = jnp.moveaxis(pair_parts, 0, 2).reshape(2, node_rows, col_count * feat_dev)
    feat_full = pair_full[0]
    grad_full = pair_full[1]
    preact = jnp.dot(agg_full, weight, preferred_element_type=jnp.float32) + jnp.dot(
        feat_full, root_weight, preferred_element_type=jnp.float32
    )
    preact_own = lax.dynamic_slice_in_dim(preact, col_index * feat_dev, feat_dev, 1)
    activations = jax.nn.silu(preact_own).astype(jnp.bfloat16)
    preact_grad = (grad_full.astype(jnp.float32) * silu_grad(preact)).astype(jnp.bfloat16)

    contract_rows = (((0,), (0,)), ((), ()))
    weight_part = lax.dot_general(
        aggregated, preact_grad, contract_rows, preferred_element_type=jnp.float32
    )
    root_part = lax.dot_general(
        features, preact_grad, contract_rows, preferred_element_type=jnp.float32
    )
    grad_scale = 1.0 / math.sqrt(nodes)
    both = jnp.concatenate([weight_part, root_part], axis=0) * grad_scale
    both_sum = reduce_rows(both.astype(jnp.bfloat16), "row", row_count)
    sum_lanes = both_sum.size // block_edge
    sum_pair = both_sum.astype(jnp.bfloat16).reshape(sum_lanes, block_edge)

    w_rows = lax.dynamic_slice_in_dim(weight, col_index * feat_dev, feat_dev, 0)
    r_rows = lax.dynamic_slice_in_dim(root_weight, col_index * feat_dev, feat_dev, 0)
    contract_cols = (((1,), (1,)), ((), ()))
    aggregated_grad = lax.dot_general(
        preact_grad, w_rows, contract_cols, preferred_element_type=jnp.float32
    ).astype(jnp.bfloat16)
    own_grad = lax.dot_general(
        preact_grad, r_rows, contract_cols, preferred_element_type=jnp.float32
    )
    column_terms = jnp.dot(dense_t, aggregated_grad, preferred_element_type=jnp.float32)
    term_pieces = column_terms.astype(jnp.bfloat16).reshape(row_count, node_rows, feat_dev)
    room = jnp.zeros((row_count,) + sum_pair.shape, term_pieces.dtype)
    outgoing = jnp.concatenate([term_pieces, room], axis=1)
    outgoing, own_grad = lax.optimization_barrier((outgoing, own_grad))
    outgoing = lax.dynamic_update_slice(
        outgoing, jnp.broadcast_to(sum_pair[None], room.shape), (0, node_rows, 0)
    )
    incoming = lax.all_to_all(outgoing, "row", 0, 0, tiled=True)
    summed_cols = incoming[:, :node_rows].astype(jnp.float32).sum(0)
    got_sums = incoming[:, node_rows:].astype(jnp.float32)
    half = row_count // 2
    weight_sum = got_sums[:half].reshape(feat_dev, -1)
    root_sum = got_sums[half:].reshape(feat_dev, -1)
    feature_grad = summed_cols + own_grad
    return (activations, feature_grad, weight_sum, root_sum)


def solution(mesh):
    in_specs = (
        P("row", "col"),
        P("row", "col"),
        P(),
        P(),
        P("row", "col", None, None, None),
        P("row", "col", None),
        P("row", "col"),
    )
    out_specs = (P("row", "col"), P("row", "col"), P("col", None), P("col", None))
    return jax.shard_map(
        per_device, mesh=mesh, in_specs=in_specs, out_specs=out_specs, check_vma=False
    )
```

```python
import math

import jax
import jax.numpy as jnp
from jax import lax
from jax.sharding import PartitionSpec as P


def silu_grad(preact):
    sig = jax.nn.sigmoid(preact)
    return sig * (1.0 + preact * (1.0 - sig))


def gather_rows(block, axis_name, parts):
    spread = jnp.broadcast_to(block[None], (parts,) + block.shape)
    got = lax.all_to_all(spread, axis_name, 0, 0, tiled=True)
    return got.reshape((parts * block.shape[0],) + block.shape[1:])


def reduce_rows(block, axis_name, parts):
    pieces = block.reshape((parts, block.shape[0] // parts) + block.shape[1:])
    got = lax.all_to_all(pieces, axis_name, 0, 0, tiled=True)
    return got.astype(jnp.float32).sum(0)


def per_device(features, grad_out, weight, root_weight, values, positions, counts):
    node_rows, feat_dev = features.shape
    slots, block_edge = values.shape[2], values.shape[-1]
    row_blocks = node_rows // block_edge
    col_count = lax.axis_size("col")
    row_count = lax.axis_size("row")
    col_index = lax.axis_index("col")

    live = (jnp.arange(slots, dtype=jnp.int32) < counts[0, 0]).astype(values.dtype)
    own_vals = (values[0, 0] * live[:, None, None]).reshape(slots * block_edge, block_edge)
    pos_row = jnp.zeros((16, block_edge), values.dtype)
    pos_row = lax.dynamic_update_slice(
        pos_row, positions[0, 0].astype(values.dtype).reshape(1, slots), (0, 0)
    )
    packed = jnp.concatenate([own_vals, pos_row, features, grad_out], axis=0)
    all_packed = lax.all_gather(packed, "col", axis=0, tiled=True).reshape(
        col_count, packed.shape[0], block_edge
    )
    tile_vals = all_packed[:, : slots * block_edge].reshape(
        col_count, slots, block_edge, block_edge
    )
    tile_pos = all_packed[:, slots * block_edge, :slots].astype(jnp.int32)
    cb = row_count * node_rows // col_count // block_edge
    n_pos = row_blocks * cb
    onehot = (tile_pos[:, :, None] == jnp.arange(n_pos, dtype=jnp.int32)[None, None, :]).astype(
        values.dtype
    )
    dense = jnp.einsum(
        "tsp,tsij->tpij", onehot, tile_vals, preferred_element_type=jnp.float32
    ).astype(values.dtype)
    dense = dense.reshape(col_count, row_blocks, cb, block_edge, block_edge)

    x_all = gather_rows(features, "row", row_count)
    x_tiles = x_all.reshape(col_count, cb, block_edge, feat_dev)
    row_hot = (
        (tile_pos // cb)[:, :, None] == jnp.arange(row_blocks, dtype=jnp.int32)[None, None, :]
    ).astype(jnp.float32)
    chosen = jnp.take_along_axis(x_tiles, (tile_pos % cb)[:, :, None, None], axis=1)
    products = jnp.einsum(
        "tsij,tsjf->tsif", tile_vals, chosen, preferred_element_type=jnp.float32
    )
    agg_f32 = jnp.sum(products[:, :, None] * row_hot[:, :, :, None, None], axis=(0, 1))
    aggregated = agg_f32.reshape(node_rows, feat_dev).astype(jnp.bfloat16)

    agg_parts = gather_rows(aggregated, "col", col_count).reshape(col_count, node_rows, feat_dev)
    nodes = row_count * node_rows
    dense_t = jnp.transpose(dense, (0, 2, 4, 1, 3)).reshape(nodes, node_rows)
    agg_parts, dense_t = lax.optimization_barrier((agg_parts, dense_t))
    agg_full = jnp.moveaxis(agg_parts, 0, 1).reshape(node_rows, col_count * feat_dev)
    pair_parts = all_packed[:, slots * block_edge + 16 :].reshape(
        col_count, 2, node_rows, feat_dev
    )
    pair_full = jnp.moveaxis(pair_parts, 0, 2).reshape(2, node_rows, col_count * feat_dev)
    feat_full = pair_full[0]
    grad_full = pair_full[1]
    preact = jnp.dot(agg_full, weight, preferred_element_type=jnp.float32) + jnp.dot(
        feat_full, root_weight, preferred_element_type=jnp.float32
    )
    preact_own = lax.dynamic_slice_in_dim(preact, col_index * feat_dev, feat_dev, 1)
    activations = jax.nn.silu(preact_own).astype(jnp.bfloat16)
    preact_grad = (grad_full.astype(jnp.float32) * silu_grad(preact)).astype(jnp.bfloat16)

    contract_rows = (((0,), (0,)), ((), ()))
    weight_part = lax.dot_general(
        aggregated, preact_grad, contract_rows, preferred_element_type=jnp.float32
    )
    root_part = lax.dot_general(
        features, preact_grad, contract_rows, preferred_element_type=jnp.float32
    )
    grad_scale = 1.0 / math.sqrt(nodes)
    both = jnp.concatenate([weight_part, root_part], axis=0) * grad_scale
    both_sum = reduce_rows(both.astype(jnp.bfloat16), "row", row_count)
    sum_lanes = both_sum.size // block_edge
    sum_pair = both_sum.astype(jnp.bfloat16).reshape(sum_lanes, block_edge)

    w_rows = lax.dynamic_slice_in_dim(weight, col_index * feat_dev, feat_dev, 0)
    r_rows = lax.dynamic_slice_in_dim(root_weight, col_index * feat_dev, feat_dev, 0)
    contract_cols = (((1,), (1,)), ((), ()))
    aggregated_grad = lax.dot_general(
        preact_grad, w_rows, contract_cols, preferred_element_type=jnp.float32
    ).astype(jnp.bfloat16)
    own_grad = lax.dot_general(
        preact_grad, r_rows, contract_cols, preferred_element_type=jnp.float32
    )
    column_terms = jnp.dot(dense_t, aggregated_grad, preferred_element_type=jnp.float32)
    term_pieces = column_terms.astype(jnp.bfloat16).reshape(row_count, node_rows, feat_dev)
    room = jnp.zeros((row_count,) + sum_pair.shape, term_pieces.dtype)
    outgoing = jnp.concatenate([term_pieces, room], axis=1)
    outgoing, own_grad = lax.optimization_barrier((outgoing, own_grad))
    outgoing = lax.dynamic_update_slice(
        outgoing, jnp.broadcast_to(sum_pair[None], room.shape), (0, node_rows, 0)
    )
    incoming = lax.all_to_all(outgoing, "row", 0, 0, tiled=True)
    summed_cols = incoming[:, :node_rows].astype(jnp.float32).sum(0)
    got_sums = incoming[:, node_rows:].astype(jnp.float32)
    half = row_count // 2
    weight_sum = got_sums[:half].reshape(feat_dev, -1)
    root_sum = got_sums[half:].reshape(feat_dev, -1)
    feature_grad = summed_cols + own_grad
    return (activations, feature_grad, weight_sum, root_sum)


def solution(mesh):
    in_specs = (
        P("row", "col"),
        P("row", "col"),
        P(),
        P(),
        P("row", "col", None, None, None),
        P("row", "col", None),
        P("row", "col"),
    )
    out_specs = (P("row", "col"), P("row", "col"), P("col", None), P("col", None))
    return jax.shard_map(
        per_device, mesh=mesh, in_specs=in_specs, out_specs=out_specs, check_vma=False
    )
```

```python
import math

import jax
import jax.numpy as jnp
from jax import lax
from jax.sharding import PartitionSpec as P


def silu_grad(preact):
    sig = jax.nn.sigmoid(preact)
    return sig * (1.0 + preact * (1.0 - sig))


def gather_rows(block, axis_name, parts):
    spread = jnp.broadcast_to(block[None], (parts,) + block.shape)
    got = lax.all_to_all(spread, axis_name, 0, 0, tiled=True)
    return got.reshape((parts * block.shape[0],) + block.shape[1:])


def reduce_rows(block, axis_name, parts):
    pieces = block.reshape((parts, block.shape[0] // parts) + block.shape[1:])
    got = lax.all_to_all(pieces, axis_name, 0, 0, tiled=True)
    return got.astype(jnp.float32).sum(0)


def per_device(features, grad_out, weight, root_weight, values, positions, counts):
    node_rows, feat_dev = features.shape
    slots, block_edge = values.shape[2], values.shape[-1]
    row_blocks = node_rows // block_edge
    col_count = lax.axis_size("col")
    row_count = lax.axis_size("row")
    col_index = lax.axis_index("col")

    live = (jnp.arange(slots, dtype=jnp.int32) < counts[0, 0]).astype(values.dtype)
    own_vals = (values[0, 0] * live[:, None, None]).reshape(slots * block_edge, block_edge)
    pos_row = jnp.zeros((16, block_edge), values.dtype)
    pos_row = lax.dynamic_update_slice(
        pos_row, positions[0, 0].astype(values.dtype).reshape(1, slots), (0, 0)
    )
    packed = jnp.concatenate([own_vals, pos_row, features, grad_out], axis=0)
    all_packed = lax.all_gather(packed, "col", axis=0, tiled=True).reshape(
        col_count, packed.shape[0], block_edge
    )
    tile_vals = all_packed[:, : slots * block_edge].reshape(
        col_count, slots, block_edge, block_edge
    )
    tile_pos = all_packed[:, slots * block_edge, :slots].astype(jnp.int32)
    cb = row_count * node_rows // col_count // block_edge
    n_pos = row_blocks * cb
    onehot = (tile_pos[:, :, None] == jnp.arange(n_pos, dtype=jnp.int32)[None, None, :]).astype(
        values.dtype
    )
    dense = jnp.einsum(
        "tsp,tsij->tpij", onehot, tile_vals, preferred_element_type=jnp.float32
    ).astype(values.dtype)
    dense = dense.reshape(col_count, row_blocks, cb, block_edge, block_edge)

    x_all = gather_rows(features, "row", row_count)
    x_tiles = x_all.reshape(col_count, cb, block_edge, feat_dev)
    col_hot = (
        (tile_pos % cb)[:, :, None] == jnp.arange(cb, dtype=jnp.int32)[None, None, :]
    ).astype(values.dtype)
    row_hot = (
        (tile_pos // cb)[:, :, None] == jnp.arange(row_blocks, dtype=jnp.int32)[None, None, :]
    ).astype(jnp.float32)
    chosen = jnp.einsum(
        "tsc,tcjf->tsjf", col_hot, x_tiles, preferred_element_type=jnp.float32
    ).astype(values.dtype)
    products = jnp.einsum(
        "tsij,tsjf->tsif", tile_vals, chosen, preferred_element_type=jnp.float32
    )
    agg_f32 = jnp.einsum("tsr,tsif->rif", row_hot, products, precision=lax.Precision.HIGHEST)
    aggregated = agg_f32.reshape(node_rows, feat_dev).astype(jnp.bfloat16)

    agg_parts = gather_rows(aggregated, "col", col_count).reshape(col_count, node_rows, feat_dev)
    nodes = row_count * node_rows
    dense_t = jnp.transpose(dense, (0, 2, 4, 1, 3)).reshape(nodes, node_rows)
    agg_parts, dense_t = lax.optimization_barrier((agg_parts, dense_t))
    agg_full = jnp.moveaxis(agg_parts, 0, 1).reshape(node_rows, col_count * feat_dev)
    pair_parts = all_packed[:, slots * block_edge + 16 :].reshape(
        col_count, 2, node_rows, feat_dev
    )
    pair_full = jnp.moveaxis(pair_parts, 0, 2).reshape(2, node_rows, col_count * feat_dev)
    feat_full = pair_full[0]
    grad_full = pair_full[1]
    preact = jnp.dot(agg_full, weight, preferred_element_type=jnp.float32) + jnp.dot(
        feat_full, root_weight, preferred_element_type=jnp.float32
    )
    preact_own = lax.dynamic_slice_in_dim(preact, col_index * feat_dev, feat_dev, 1)
    activations = jax.nn.silu(preact_own).astype(jnp.bfloat16)
    preact_grad = (grad_full.astype(jnp.float32) * silu_grad(preact)).astype(jnp.bfloat16)

    contract_rows = (((0,), (0,)), ((), ()))
    weight_part = lax.dot_general(
        aggregated, preact_grad, contract_rows, preferred_element_type=jnp.float32
    )
    root_part = lax.dot_general(
        features, preact_grad, contract_rows, preferred_element_type=jnp.float32
    )
    grad_scale = 1.0 / math.sqrt(nodes)
    both = jnp.concatenate([weight_part, root_part], axis=0) * grad_scale
    both_sum = reduce_rows(both.astype(jnp.bfloat16), "row", row_count)
    sum_rows, sum_cols = both_sum.shape
    lane_tiles = sum_cols // block_edge
    sum_lanes = both_sum.size // block_edge
    sum_pair = (
        both_sum.astype(jnp.bfloat16)
        .reshape(sum_rows, lane_tiles, block_edge)
        .transpose(1, 0, 2)
        .reshape(sum_lanes, block_edge)
    )

    w_rows = lax.dynamic_slice_in_dim(weight, col_index * feat_dev, feat_dev, 0)
    r_rows = lax.dynamic_slice_in_dim(root_weight, col_index * feat_dev, feat_dev, 0)
    contract_cols = (((1,), (1,)), ((), ()))
    aggregated_grad = lax.dot_general(
        preact_grad, w_rows, contract_cols, preferred_element_type=jnp.float32
    ).astype(jnp.bfloat16)
    own_grad = lax.dot_general(
        preact_grad, r_rows, contract_cols, preferred_element_type=jnp.float32
    )
    column_terms = jnp.dot(dense_t, aggregated_grad, preferred_element_type=jnp.float32)
    term_pieces = column_terms.astype(jnp.bfloat16).reshape(row_count, node_rows, feat_dev)
    room = jnp.zeros((row_count,) + sum_pair.shape, term_pieces.dtype)
    outgoing = jnp.concatenate([term_pieces, room], axis=1)
    outgoing, own_grad = lax.optimization_barrier((outgoing, own_grad))
    outgoing = lax.dynamic_update_slice(
        outgoing, jnp.broadcast_to(sum_pair[None], room.shape), (0, node_rows, 0)
    )
    incoming = lax.all_to_all(outgoing, "row", 0, 0, tiled=True)
    summed_cols = incoming[:, :node_rows].astype(jnp.float32).sum(0)
    got_sums = (
        incoming[:, node_rows:]
        .reshape(row_count, lane_tiles, sum_rows, block_edge)
        .transpose(0, 2, 1, 3)
        .astype(jnp.float32)
    )
    half = row_count // 2
    weight_sum = got_sums[:half].reshape(feat_dev, -1)
    root_sum = got_sums[half:].reshape(feat_dev, -1)
    feature_grad = summed_cols + own_grad
    return (activations, feature_grad, weight_sum, root_sum)


def solution(mesh):
    in_specs = (
        P("row", "col"),
        P("row", "col"),
        P(),
        P(),
        P("row", "col", None, None, None),
        P("row", "col", None),
        P("row", "col"),
    )
    out_specs = (P("row", "col"), P("row", "col"), P("col", None), P("col", None))
    return jax.shard_map(
        per_device, mesh=mesh, in_specs=in_specs, out_specs=out_specs, check_vma=False
    )
```

```python
import math

import jax
import jax.numpy as jnp
from jax import lax
from jax.sharding import PartitionSpec as P


def silu_grad(preact):
    sig = jax.nn.sigmoid(preact)
    return sig * (1.0 + preact * (1.0 - sig))


def gather_rows(block, axis_name, parts):
    spread = jnp.broadcast_to(block[None], (parts,) + block.shape)
    got = lax.all_to_all(spread, axis_name, 0, 0, tiled=True)
    return got.reshape((parts * block.shape[0],) + block.shape[1:])


def reduce_rows(block, axis_name, parts):
    pieces = block.reshape((parts, block.shape[0] // parts) + block.shape[1:])
    got = lax.all_to_all(pieces, axis_name, 0, 0, tiled=True)
    return got.astype(jnp.float32).sum(0)


def per_device(features, grad_out, weight, root_weight, values, positions, counts):
    node_rows, feat_dev = features.shape
    slots, block_edge = values.shape[2], values.shape[-1]
    row_blocks = node_rows // block_edge
    col_count = lax.axis_size("col")
    row_count = lax.axis_size("row")
    col_index = lax.axis_index("col")

    live = (jnp.arange(slots, dtype=jnp.int32) < counts[0, 0]).astype(values.dtype)
    own_vals = (values[0, 0] * live[:, None, None]).reshape(slots * block_edge, block_edge)
    pos_row = jnp.zeros((16, block_edge), values.dtype)
    pos_row = lax.dynamic_update_slice(
        pos_row, positions[0, 0].astype(values.dtype).reshape(1, slots), (0, 0)
    )
    packed = jnp.concatenate([own_vals, pos_row, features, grad_out], axis=0)
    all_packed = lax.all_gather(packed, "col", axis=0, tiled=True).reshape(
        col_count, packed.shape[0], block_edge
    )
    tile_vals = all_packed[:, : slots * block_edge].reshape(
        col_count, slots, block_edge, block_edge
    )
    tile_pos = all_packed[:, slots * block_edge, :slots].astype(jnp.int32)
    cb = row_count * node_rows // col_count // block_edge
    n_pos = row_blocks * cb
    onehot = (tile_pos[:, :, None] == jnp.arange(n_pos, dtype=jnp.int32)[None, None, :]).astype(
        values.dtype
    )
    dense = jnp.einsum(
        "tsp,tsij->tpij", onehot, tile_vals, preferred_element_type=jnp.float32
    ).astype(values.dtype)
    dense = dense.reshape(col_count, row_blocks, cb, block_edge, block_edge)

    x_all = gather_rows(features, "row", row_count)
    x_tiles = x_all.reshape(col_count, cb, block_edge, feat_dev)
    col_hot = (
        (tile_pos % cb)[:, :, None] == jnp.arange(cb, dtype=jnp.int32)[None, None, :]
    ).astype(values.dtype)
    row_hot = (
        (tile_pos // cb)[:, :, None] == jnp.arange(row_blocks, dtype=jnp.int32)[None, None, :]
    ).astype(jnp.float32)
    chosen = jnp.einsum(
        "tsc,tcjf->tsjf", col_hot, x_tiles, preferred_element_type=jnp.float32
    ).astype(values.dtype)
    products = jnp.einsum(
        "tsij,tsjf->tsif", tile_vals, chosen, preferred_element_type=jnp.float32
    )
    agg_f32 = jnp.sum(products[:, :, None] * row_hot[:, :, :, None, None], axis=(0, 1))
    aggregated = agg_f32.reshape(node_rows, feat_dev).astype(jnp.bfloat16)

    agg_parts = gather_rows(aggregated, "col", col_count).reshape(col_count, node_rows, feat_dev)
    nodes = row_count * node_rows
    dense_t = jnp.transpose(dense, (0, 2, 4, 1, 3)).reshape(nodes, node_rows)
    agg_parts, dense_t = lax.optimization_barrier((agg_parts, dense_t))
    agg_full = jnp.moveaxis(agg_parts, 0, 1).reshape(node_rows, col_count * feat_dev)
    pair_parts = all_packed[:, slots * block_edge + 16 :].reshape(
        col_count, 2, node_rows, feat_dev
    )
    pair_full = jnp.moveaxis(pair_parts, 0, 2).reshape(2, node_rows, col_count * feat_dev)
    feat_full = pair_full[0]
    grad_full = pair_full[1]
    preact = jnp.dot(agg_full, weight, preferred_element_type=jnp.float32) + jnp.dot(
        feat_full, root_weight, preferred_element_type=jnp.float32
    )
    preact_own = lax.dynamic_slice_in_dim(preact, col_index * feat_dev, feat_dev, 1)
    activations = jax.nn.silu(preact_own).astype(jnp.bfloat16)
    preact_grad = (grad_full.astype(jnp.float32) * silu_grad(preact)).astype(jnp.bfloat16)

    contract_rows = (((0,), (0,)), ((), ()))
    weight_part = lax.dot_general(
        aggregated, preact_grad, contract_rows, preferred_element_type=jnp.float32
    )
    root_part = lax.dot_general(
        features, preact_grad, contract_rows, preferred_element_type=jnp.float32
    )
    grad_scale = 1.0 / math.sqrt(nodes)
    both = jnp.concatenate([weight_part, root_part], axis=0) * grad_scale
    both_sum = reduce_rows(both.astype(jnp.bfloat16), "row", row_count)
    sum_rows, sum_cols = both_sum.shape
    lane_tiles = sum_cols // block_edge
    sum_lanes = both_sum.size // block_edge
    sum_pair = (
        both_sum.astype(jnp.bfloat16)
        .reshape(sum_rows, lane_tiles, block_edge)
        .transpose(1, 0, 2)
        .reshape(sum_lanes, block_edge)
    )

    w_rows = lax.dynamic_slice_in_dim(weight, col_index * feat_dev, feat_dev, 0)
    r_rows = lax.dynamic_slice_in_dim(root_weight, col_index * feat_dev, feat_dev, 0)
    contract_cols = (((1,), (1,)), ((), ()))
    aggregated_grad = lax.dot_general(
        preact_grad, w_rows, contract_cols, preferred_element_type=jnp.float32
    ).astype(jnp.bfloat16)
    own_grad = lax.dot_general(
        preact_grad, r_rows, contract_cols, preferred_element_type=jnp.float32
    )
    column_terms = jnp.dot(dense_t, aggregated_grad, preferred_element_type=jnp.float32)
    term_pieces = column_terms.astype(jnp.bfloat16).reshape(row_count, node_rows, feat_dev)
    room = jnp.zeros((row_count,) + sum_pair.shape, term_pieces.dtype)
    outgoing = jnp.concatenate([term_pieces, room], axis=1)
    outgoing, own_grad = lax.optimization_barrier((outgoing, own_grad))
    outgoing = lax.dynamic_update_slice(
        outgoing, jnp.broadcast_to(sum_pair[None], room.shape), (0, node_rows, 0)
    )
    incoming = lax.all_to_all(outgoing, "row", 0, 0, tiled=True)
    summed_cols = incoming[:, :node_rows].astype(jnp.float32).sum(0)
    got_sums = (
        incoming[:, node_rows:]
        .reshape(row_count, lane_tiles, sum_rows, block_edge)
        .transpose(0, 2, 1, 3)
        .astype(jnp.float32)
    )
    half = row_count // 2
    weight_sum = got_sums[:half].reshape(feat_dev, -1)
    root_sum = got_sums[half:].reshape(feat_dev, -1)
    feature_grad = summed_cols + own_grad
    return (activations, feature_grad, weight_sum, root_sum)


def solution(mesh):
    in_specs = (
        P("row", "col"),
        P("row", "col"),
        P(),
        P(),
        P("row", "col", None, None, None),
        P("row", "col", None),
        P("row", "col"),
    )
    out_specs = (P("row", "col"), P("row", "col"), P("col", None), P("col", None))
    return jax.shard_map(
        per_device, mesh=mesh, in_specs=in_specs, out_specs=out_specs, check_vma=False
    )
```

```python
import math

import jax
import jax.numpy as jnp
from jax import lax
from jax.sharding import PartitionSpec as P


def silu_grad(preact):
    sig = jax.nn.sigmoid(preact)
    return sig * (1.0 + preact * (1.0 - sig))


def gather_rows(block, axis_name, parts):
    spread = jnp.broadcast_to(block[None], (parts,) + block.shape)
    got = lax.all_to_all(spread, axis_name, 0, 0, tiled=True)
    return got.reshape((parts * block.shape[0],) + block.shape[1:])


def reduce_rows(block, axis_name, parts):
    pieces = block.reshape((parts, block.shape[0] // parts) + block.shape[1:])
    got = lax.all_to_all(pieces, axis_name, 0, 0, tiled=True)
    return got.astype(jnp.float32).sum(0)


def per_device(features, grad_out, weight, root_weight, values, positions, counts):
    node_rows, feat_dev = features.shape
    slots, block_edge = values.shape[2], values.shape[-1]
    row_blocks = node_rows // block_edge
    col_count = lax.axis_size("col")
    row_count = lax.axis_size("row")
    col_index = lax.axis_index("col")

    live = (jnp.arange(slots, dtype=jnp.int32) < counts[0, 0]).astype(values.dtype)
    own_vals = (values[0, 0] * live[:, None, None]).reshape(slots * block_edge, block_edge)
    pos_row = jnp.zeros((16, block_edge), values.dtype)
    pos_row = lax.dynamic_update_slice(
        pos_row, positions[0, 0].astype(values.dtype).reshape(1, slots), (0, 0)
    )
    packed = jnp.concatenate([own_vals, pos_row, features, grad_out], axis=0)
    all_packed = lax.all_gather(packed, "col", axis=0, tiled=True).reshape(
        col_count, packed.shape[0], block_edge
    )
    tile_vals = all_packed[:, : slots * block_edge].reshape(
        col_count, slots, block_edge, block_edge
    )
    tile_pos = all_packed[:, slots * block_edge, :slots].astype(jnp.int32)
    cb = row_count * node_rows // col_count // block_edge
    n_pos = row_blocks * cb
    onehot = (tile_pos[:, :, None] == jnp.arange(n_pos, dtype=jnp.int32)[None, None, :]).astype(
        values.dtype
    )
    dense = jnp.einsum(
        "tsp,tsij->tpij", onehot, tile_vals, preferred_element_type=jnp.float32
    ).astype(values.dtype)
    dense = dense.reshape(col_count, row_blocks, cb, block_edge, block_edge)

    x_all = gather_rows(features, "row", row_count)
    x_tiles = x_all.reshape(col_count, cb, block_edge, feat_dev)
    col_hot = (
        (tile_pos % cb)[:, :, None] == jnp.arange(cb, dtype=jnp.int32)[None, None, :]
    ).astype(values.dtype)
    row_hot = (
        (tile_pos // cb)[:, :, None] == jnp.arange(row_blocks, dtype=jnp.int32)[None, None, :]
    ).astype(jnp.float32)
    chosen = jnp.einsum(
        "tsc,tcjf->tsjf", col_hot, x_tiles, preferred_element_type=jnp.float32
    ).astype(values.dtype)
    products = jnp.einsum(
        "tsij,tsjf->tsif", tile_vals, chosen, preferred_element_type=jnp.float32
    )
    agg_f32 = jnp.sum(products[:, :, None] * row_hot[:, :, :, None, None], axis=(0, 1))
    aggregated = agg_f32.reshape(node_rows, feat_dev).astype(jnp.bfloat16)

    agg_parts = gather_rows(aggregated, "col", col_count).reshape(col_count, node_rows, feat_dev)
    nodes = row_count * node_rows
    dense_t = jnp.transpose(dense, (0, 2, 4, 1, 3)).reshape(nodes, node_rows)
    agg_parts, dense_t = lax.optimization_barrier((agg_parts, dense_t))
    agg_full = jnp.moveaxis(agg_parts, 0, 1).reshape(node_rows, col_count * feat_dev)
    pair_parts = all_packed[:, slots * block_edge + 16 :].reshape(
        col_count, 2, node_rows, feat_dev
    )
    pair_full = jnp.moveaxis(pair_parts, 0, 2).reshape(2, node_rows, col_count * feat_dev)
    feat_full = pair_full[0]
    grad_full = pair_full[1]
    preact = jnp.dot(agg_full, weight, preferred_element_type=jnp.float32) + jnp.dot(
        feat_full, root_weight, preferred_element_type=jnp.float32
    )
    preact_own = lax.dynamic_slice_in_dim(preact, col_index * feat_dev, feat_dev, 1)
    activations = jax.nn.silu(preact_own).astype(jnp.bfloat16)
    preact_grad = (grad_full.astype(jnp.float32) * silu_grad(preact)).astype(jnp.bfloat16)

    contract_rows = (((0,), (0,)), ((), ()))
    weight_part = lax.dot_general(
        aggregated, preact_grad, contract_rows, preferred_element_type=jnp.float32
    )
    root_part = lax.dot_general(
        features, preact_grad, contract_rows, preferred_element_type=jnp.float32
    )
    grad_scale = 1.0 / math.sqrt(nodes)
    both = jnp.concatenate([weight_part, root_part], axis=0) * grad_scale
    sum_rows = both.shape[0] // row_count
    lane_tiles = both.shape[1] // block_edge
    sum_lanes = sum_rows * lane_tiles
    both_tiled = (
        both.astype(jnp.bfloat16)
        .reshape(row_count, sum_rows, lane_tiles, block_edge)
        .transpose(0, 2, 1, 3)
        .reshape(row_count * sum_lanes, block_edge)
    )
    sum_pair = reduce_rows(both_tiled, "row", row_count).astype(jnp.bfloat16)

    w_rows = lax.dynamic_slice_in_dim(weight, col_index * feat_dev, feat_dev, 0)
    r_rows = lax.dynamic_slice_in_dim(root_weight, col_index * feat_dev, feat_dev, 0)
    contract_cols = (((1,), (1,)), ((), ()))
    aggregated_grad = lax.dot_general(
        preact_grad, w_rows, contract_cols, preferred_element_type=jnp.float32
    ).astype(jnp.bfloat16)
    own_grad = lax.dot_general(
        preact_grad, r_rows, contract_cols, preferred_element_type=jnp.float32
    )
    column_terms = jnp.dot(dense_t, aggregated_grad, preferred_element_type=jnp.float32)
    term_pieces = column_terms.astype(jnp.bfloat16).reshape(row_count, node_rows, feat_dev)
    room = jnp.zeros((row_count,) + sum_pair.shape, term_pieces.dtype)
    outgoing = jnp.concatenate([term_pieces, room], axis=1)
    outgoing, own_grad = lax.optimization_barrier((outgoing, own_grad))
    outgoing = lax.dynamic_update_slice(
        outgoing, jnp.broadcast_to(sum_pair[None], room.shape), (0, node_rows, 0)
    )
    incoming = lax.all_to_all(outgoing, "row", 0, 0, tiled=True)
    summed_cols = incoming[:, :node_rows].astype(jnp.float32).sum(0)
    got_sums = (
        incoming[:, node_rows:]
        .reshape(row_count, lane_tiles, sum_rows, block_edge)
        .transpose(0, 2, 1, 3)
        .astype(jnp.float32)
    )
    half = row_count // 2
    weight_sum = got_sums[:half].reshape(feat_dev, -1)
    root_sum = got_sums[half:].reshape(feat_dev, -1)
    feature_grad = summed_cols + own_grad
    return (activations, feature_grad, weight_sum, root_sum)


def solution(mesh):
    in_specs = (
        P("row", "col"),
        P("row", "col"),
        P(),
        P(),
        P("row", "col", None, None, None),
        P("row", "col", None),
        P("row", "col"),
    )
    out_specs = (P("row", "col"), P("row", "col"), P("col", None), P("col", None))
    return jax.shard_map(
        per_device, mesh=mesh, in_specs=in_specs, out_specs=out_specs, check_vma=False
    )
```

```python
import math

import jax
import jax.numpy as jnp
from jax import lax
from jax.sharding import PartitionSpec as P


def silu_grad(preact):
    sig = jax.nn.sigmoid(preact)
    return sig * (1.0 + preact * (1.0 - sig))


def gather_rows(block, axis_name, parts):
    spread = jnp.broadcast_to(block[None], (parts,) + block.shape)
    got = lax.all_to_all(spread, axis_name, 0, 0, tiled=True)
    return got.reshape((parts * block.shape[0],) + block.shape[1:])


def reduce_rows(block, axis_name, parts):
    pieces = block.reshape((parts, block.shape[0] // parts) + block.shape[1:])
    got = lax.all_to_all(pieces, axis_name, 0, 0, tiled=True)
    return got.astype(jnp.float32).sum(0)


def per_device(features, grad_out, weight, root_weight, values, positions, counts):
    node_rows, feat_dev = features.shape
    slots, block_edge = values.shape[2], values.shape[-1]
    row_blocks = node_rows // block_edge
    col_count = lax.axis_size("col")
    row_count = lax.axis_size("row")
    col_index = lax.axis_index("col")

    live = (jnp.arange(slots, dtype=jnp.int32) < counts[0, 0]).astype(values.dtype)
    own_vals = (values[0, 0] * live[:, None, None]).reshape(slots * block_edge, block_edge)
    pos_row = jnp.zeros((block_edge, block_edge), values.dtype)
    pos_row = lax.dynamic_update_slice(
        pos_row, positions[0, 0].astype(values.dtype).reshape(1, slots), (0, 0)
    )
    packed = jnp.concatenate([own_vals, pos_row, features, grad_out], axis=0)
    all_packed = lax.all_gather(packed, "col", axis=0, tiled=True).reshape(
        col_count, packed.shape[0], block_edge
    )
    tile_vals = all_packed.reshape(col_count, -1, block_edge, block_edge)[:, :slots]
    tile_pos = all_packed[:, slots * block_edge, :slots].astype(jnp.int32)
    cb = row_count * node_rows // col_count // block_edge
    n_pos = row_blocks * cb
    onehot = (tile_pos[:, :, None] == jnp.arange(n_pos, dtype=jnp.int32)[None, None, :]).astype(
        values.dtype
    )
    dense = jnp.einsum(
        "tsp,tsij->tpij", onehot, tile_vals, preferred_element_type=jnp.float32
    ).astype(values.dtype)
    dense = dense.reshape(col_count, row_blocks, cb, block_edge, block_edge)

    x_all = gather_rows(features, "row", row_count)
    x_tiles = x_all.reshape(col_count, cb, block_edge, feat_dev)
    col_hot = (
        (tile_pos % cb)[:, :, None] == jnp.arange(cb, dtype=jnp.int32)[None, None, :]
    ).astype(values.dtype)
    row_hot = (
        (tile_pos // cb)[:, :, None] == jnp.arange(row_blocks, dtype=jnp.int32)[None, None, :]
    ).astype(jnp.float32)
    chosen = jnp.einsum(
        "tsc,tcjf->tsjf", col_hot, x_tiles, preferred_element_type=jnp.float32
    ).astype(values.dtype)
    products = jnp.einsum(
        "tsij,tsjf->tsif", tile_vals, chosen, preferred_element_type=jnp.float32
    )
    agg_f32 = jnp.sum(products[:, :, None] * row_hot[:, :, :, None, None], axis=(0, 1))
    aggregated = agg_f32.reshape(node_rows, feat_dev).astype(jnp.bfloat16)

    agg_parts = gather_rows(aggregated, "col", col_count).reshape(col_count, node_rows, feat_dev)
    nodes = row_count * node_rows
    dense_t = jnp.transpose(dense, (0, 2, 4, 1, 3)).reshape(nodes, node_rows)
    agg_parts, dense_t = lax.optimization_barrier((agg_parts, dense_t))
    agg_full = jnp.moveaxis(agg_parts, 0, 1).reshape(node_rows, col_count * feat_dev)
    pair_parts = all_packed[:, (slots + 1) * block_edge :].reshape(
        col_count, 2, node_rows, feat_dev
    )
    pair_full = jnp.moveaxis(pair_parts, 0, 2).reshape(2, node_rows, col_count * feat_dev)
    feat_full = pair_full[0]
    grad_full = pair_full[1]
    preact = jnp.dot(agg_full, weight, preferred_element_type=jnp.float32) + jnp.dot(
        feat_full, root_weight, preferred_element_type=jnp.float32
    )
    preact_own = lax.dynamic_slice_in_dim(preact, col_index * feat_dev, feat_dev, 1)
    activations = jax.nn.silu(preact_own).astype(jnp.bfloat16)
    preact_grad = (grad_full.astype(jnp.float32) * silu_grad(preact)).astype(jnp.bfloat16)

    contract_rows = (((0,), (0,)), ((), ()))
    weight_part = lax.dot_general(
        aggregated, preact_grad, contract_rows, preferred_element_type=jnp.float32
    )
    root_part = lax.dot_general(
        features, preact_grad, contract_rows, preferred_element_type=jnp.float32
    )
    grad_scale = 1.0 / math.sqrt(nodes)
    both = jnp.concatenate([weight_part, root_part], axis=0) * grad_scale
    sum_rows = both.shape[0] // row_count
    lane_tiles = both.shape[1] // block_edge
    sum_lanes = sum_rows * lane_tiles
    both_tiled = (
        both.astype(jnp.bfloat16)
        .reshape(row_count, sum_rows, lane_tiles, block_edge)
        .transpose(0, 2, 1, 3)
        .reshape(row_count * sum_lanes, block_edge)
    )
    sum_pair = reduce_rows(both_tiled, "row", row_count).astype(jnp.bfloat16)

    w_rows = lax.dynamic_slice_in_dim(weight, col_index * feat_dev, feat_dev, 0)
    r_rows = lax.dynamic_slice_in_dim(root_weight, col_index * feat_dev, feat_dev, 0)
    contract_cols = (((1,), (1,)), ((), ()))
    aggregated_grad = lax.dot_general(
        preact_grad, w_rows, contract_cols, preferred_element_type=jnp.float32
    ).astype(jnp.bfloat16)
    own_grad = lax.dot_general(
        preact_grad, r_rows, contract_cols, preferred_element_type=jnp.float32
    )
    column_terms = jnp.dot(dense_t, aggregated_grad, preferred_element_type=jnp.float32)
    term_pieces = column_terms.astype(jnp.bfloat16).reshape(row_count, node_rows, feat_dev)
    room = jnp.zeros((row_count,) + sum_pair.shape, term_pieces.dtype)
    outgoing = jnp.concatenate([term_pieces, room], axis=1)
    outgoing, own_grad = lax.optimization_barrier((outgoing, own_grad))
    outgoing = lax.dynamic_update_slice(
        outgoing, jnp.broadcast_to(sum_pair[None], room.shape), (0, node_rows, 0)
    )
    incoming = lax.all_to_all(outgoing, "row", 0, 0, tiled=True)
    summed_cols = incoming[:, :node_rows].astype(jnp.float32).sum(0)
    got_sums = (
        incoming[:, node_rows:]
        .reshape(row_count, lane_tiles, sum_rows, block_edge)
        .transpose(0, 2, 1, 3)
        .astype(jnp.float32)
    )
    half = row_count // 2
    weight_sum = got_sums[:half].reshape(feat_dev, -1)
    root_sum = got_sums[half:].reshape(feat_dev, -1)
    feature_grad = summed_cols + own_grad
    return (activations, feature_grad, weight_sum, root_sum)


def solution(mesh):
    in_specs = (
        P("row", "col"),
        P("row", "col"),
        P(),
        P(),
        P("row", "col", None, None, None),
        P("row", "col", None),
        P("row", "col"),
    )
    out_specs = (P("row", "col"), P("row", "col"), P("col", None), P("col", None))
    return jax.shard_map(
        per_device, mesh=mesh, in_specs=in_specs, out_specs=out_specs, check_vma=False
    )
```
